32 devices in a mesh: trait: 4 (over y, x), tile: 8 (over z, core).
Axes of the slice: x: 2, y: 2, z: 4, core: 2. Of those that a mesh axis runs over, the one named last changes fastest.
Arguments:
- probe_signs: int32 [4, 16, 64, 2048], P(None, 'trait', 'tile'), may hold values from 0 to 1
- land_mask: int32 [64, 2048], P('tile'), may hold values from 0 to 1
- kappa_sq: float32 [64, 2048], P('tile'), may hold values from 0.2 to 4.5
- trait_covariance: float32 [16, 16], replicated, may hold values from -0.025 to 3, as said below
Outputs:
- alphas: float32 [4, 3], replicated
- betas: float32 [4, 3], replicated
- last_vector: float32 [4, 16, 64, 2048], P(None, 'trait', 'tile')
The draws below stay inside these ranges and needn't reach their ends.
Inputs may be any that keep to these rules, and one draw needn't show every extreme that they name: `trait_covariance`: symmetric.
All inputs are finite; a program needn't handle non-finite values.
Results may differ from the reference program's by a relative error of at most 0.0003.
Values may be sent and summed in bfloat16 or wider, within the bound.
No kernel may reach another device: no remote copies, remote signals or barrier semaphores. Data moves between devices by JAX's collectives and lax.ppermute only.
A program may use at most 64 MiB of HBM per device.

```python
import jax
import jax.numpy as jnp
from jax import lax

TRAITS = 16
PROBES = 4
COLS = 2048
ITERS = 3
ROWS = 64


def draw_land_mask(key, part):
    rows = lax.broadcasted_iota(jnp.int32, (ROWS, COLS), 0)
    threshold = 250 + 500 * rows // max(ROWS - 1, 1)
    values = jax.random.randint(key, (ROWS, COLS), 0, 1000)
    return (values < threshold).astype(jnp.int32)


def draw_kappa_sq(key, part):
    uniform = jax.random.uniform(key, (ROWS, COLS), jnp.float32)
    return 0.2 * jnp.exp(uniform * jnp.log(7.5))


def draw_trait_covariance(key, part):
    first_key = jax.random.fold_in(key, 11)
    second_key = jax.random.fold_in(key, 23)
    jitter = jax.random.uniform(first_key, (TRAITS,), jnp.float32, 0.9, 1.1)
    position = lax.broadcasted_iota(jnp.int32, (TRAITS,), 0).astype(jnp.float32) / max(TRAITS - 1, 1)
    diagonal = 0.5 * jnp.exp(position * jnp.log(3.0)) * jitter
    offdiag = jax.random.uniform(second_key, (TRAITS, TRAITS), jnp.float32, -0.025, 0.025)
    upper = jnp.triu(offdiag, 1)
    return upper + upper.T + jnp.diag(diagonal)


def place_ends(drawn, own_key, least, largest):
    spot = [jax.random.randint(jax.random.fold_in(own_key, axis), (), 0, length) for axis, length in enumerate(drawn.shape)]
    main_axis = drawn.shape.index(max(drawn.shape))
    neighbour = spot[:main_axis] + [(spot[main_axis] + 1) % drawn.shape[main_axis]] + spot[main_axis + 1:]
    return drawn.at[tuple(spot)].set(least).at[tuple(neighbour)].set(largest)


def setup_inputs(seed: int = 0) -> dict:
    keys = jax.random.split(jax.random.key(seed), 5)
    probe_signs = place_ends(jax.random.randint(keys[0], (PROBES, TRAITS, ROWS, COLS), 0, 2), jax.random.fold_in(keys[0], 1), 0, 1).astype(jnp.int32)
    land_mask = draw_land_mask(jax.random.fold_in(keys[4], 71), 0)
    kappa_sq = draw_kappa_sq(jax.random.fold_in(keys[4], 71), 0)
    trait_covariance = draw_trait_covariance(jax.random.fold_in(keys[4], 71), 0)
    return {"probe_signs": probe_signs, "land_mask": land_mask, "kappa_sq": kappa_sq, "trait_covariance": trait_covariance}


along_cols = 0.25
along_rows = 0.15
cross_term = 0.1
epsilon = 1e-06

def nine_point(padded, kappa_rows):
    center = padded[..., 1:-1, 1:-1]
    sideways = padded[..., 1:-1, :-2] + padded[..., 1:-1, 2:]
    vertical = padded[..., :-2, 1:-1] + padded[..., 2:, 1:-1]
    diag_main = padded[..., 2:, 2:] + padded[..., :-2, :-2]
    diag_anti = padded[..., 2:, :-2] + padded[..., :-2, 2:]
    return (kappa_rows + 2.0 * along_cols + 2.0 * along_rows) * center - along_cols * sideways - along_rows * vertical - 0.5 * cross_term * (diag_main - diag_anti)

def operate(field, covariance, land, kappa_sq):
    widths = ((0, 0), (0, 0), (1, 1), (1, 1))
    mixed = jnp.einsum('ts,psrc->ptrc', covariance, field, precision=lax.Precision.HIGHEST)
    first = land * nine_point(jnp.pad(mixed, widths), kappa_sq)
    return land * nine_point(jnp.pad(first, widths), kappa_sq)

def reference(probe_signs, land_mask, kappa_sq, trait_covariance):
    land = land_mask.astype(jnp.float32)
    variances = jnp.diagonal(trait_covariance)
    start_field = land * (2 * probe_signs - 1).astype(jnp.float32) * variances[None, :, None, None]
    norm = jnp.sqrt(lax.optimization_barrier(jnp.sum(start_field * start_field, axis=(1, 2, 3))) + epsilon)
    current = start_field / norm[:, None, None, None]
    previous = jnp.zeros_like(current)
    beta_prev = jnp.zeros((PROBES,), jnp.float32)
    alpha_list = []
    beta_list = []
    for step in range(ITERS):
        image = operate(current, trait_covariance, land, kappa_sq) - beta_prev[:, None, None, None] * previous
        alpha = lax.optimization_barrier(jnp.sum(image * current, axis=(1, 2, 3)))
        residual = image - alpha[:, None, None, None] * current
        beta = jnp.sqrt(lax.optimization_barrier(jnp.sum(residual * residual, axis=(1, 2, 3))) + epsilon)
        previous = current
        current = residual / beta[:, None, None, None]
        beta_prev = beta
        alpha_list.append(alpha)
        beta_list.append(beta)
    return (jnp.stack(alpha_list, axis=1), jnp.stack(beta_list, axis=1), current * norm[:, None, None, None])
```

```python
import jax
import jax.numpy as jnp
from jax import lax
from jax.sharding import PartitionSpec as P


along_cols = 0.25
along_rows = 0.15
cross_term = 0.1
epsilon = 1e-06

HALO = 6


def nine_valid(x, kappa_rows):
    padded = jnp.pad(x, [(0, 0)] * (x.ndim - 1) + [(1, 1)])
    center = padded[..., 1:-1, 1:-1]
    sideways = padded[..., 1:-1, :-2] + padded[..., 1:-1, 2:]
    vertical = padded[..., :-2, 1:-1] + padded[..., 2:, 1:-1]
    diag_main = padded[..., 2:, 2:] + padded[..., :-2, :-2]
    diag_anti = padded[..., 2:, :-2] + padded[..., :-2, 2:]
    return (
        (kappa_rows + 2.0 * along_cols + 2.0 * along_rows) * center
        - along_cols * sideways
        - along_rows * vertical
        - 0.5 * cross_term * (diag_main - diag_anti)
    )


def tile_sum(v):
    n = lax.axis_size("tile")
    if n & (n - 1):
        return lax.psum(v, "tile")
    s = 1
    while s < n:
        v = v + lax.ppermute(v, "tile", [(i, i ^ s) for i in range(n)])
        s *= 2
    return v


def halo_rows(block, width):
    n = lax.axis_size("tile")
    dim = block.ndim - 2
    rows = block.shape[dim]
    assert rows >= width
    forward = [(i, i + 1) for i in range(n - 1)]
    backward = [(i + 1, i) for i in range(n - 1)]
    low = lax.ppermute(lax.slice_in_dim(block, rows - width, rows, axis=dim), "tile", forward)
    high = lax.ppermute(lax.slice_in_dim(block, 0, width, axis=dim), "tile", backward)
    return jnp.concatenate([low, block, high], axis=dim)


def shards(probe_signs, land_mask, kappa_sq, trait_covariance):
    rows = land_mask.shape[0]
    h = HALO
    signed = (land_mask[None, None] * (2 * probe_signs - 1)).astype(jnp.bfloat16)
    exchanged = lax.all_to_all(signed, "trait", split_axis=0, concat_axis=1, tiled=True)
    field_ext = halo_rows(exchanged, h).astype(jnp.float32)
    kappa_ext = halo_rows(kappa_sq, h)
    land_ext = field_ext[0, 0] * field_ext[0, 0]
    variances = jnp.diagonal(trait_covariance)
    z = field_ext * variances[None, :, None, None]

    def apply_a(x, off):
        r = x.shape[2]
        mixed = jnp.einsum("ts,psrc->ptrc", trait_covariance, x, precision=lax.Precision.HIGHEST)
        first = land_ext[off + 1 : off + r - 1] * nine_valid(mixed, kappa_ext[off + 1 : off + r - 1])
        return land_ext[off + 2 : off + r - 2] * nine_valid(first, kappa_ext[off + 2 : off + r - 2])

    def own(x, off):
        return x[:, :, h - off : h - off + rows]

    def dot(a, b, off):
        return jnp.sum(own(a, off) * own(b, off), axis=(1, 2, 3))

    def crop(x, k):
        return x[:, :, k : x.shape[2] - k]

    az = apply_a(z, 0)
    z2 = crop(z, 2)
    sums = tile_sum(jnp.stack([dot(z2, z2, 2), dot(az, z2, 2)], axis=-1))
    norm = jnp.sqrt(sums[:, 0] + epsilon)
    alpha = sums[:, 1] / (norm * norm)
    q = z2 / norm[:, None, None, None]
    v = az / norm[:, None, None, None]
    w = v - alpha[:, None, None, None] * q
    off = 2
    alphas = [alpha]
    betas = []
    iters = 3
    for step in range(1, iters):
        aw = apply_a(w, off)
        w2 = crop(w, 2)
        q2 = crop(q, 2)
        off += 2
        sums = tile_sum(
            jnp.stack([dot(w2, w2, off), dot(aw, w2, off), dot(q2, w2, off)], axis=-1)
        )
        beta = jnp.sqrt(sums[:, 0] + epsilon)
        alpha = sums[:, 1] / (beta * beta) - sums[:, 2]
        q_next = w2 / beta[:, None, None, None]
        v = aw / beta[:, None, None, None] - beta[:, None, None, None] * q2
        w = v - alpha[:, None, None, None] * q_next
        q = q_next
        betas.append(beta)
        alphas.append(alpha)
    w_own = own(w, off)
    sums = tile_sum(jnp.sum(w_own * w_own, axis=(1, 2, 3)))
    beta = jnp.sqrt(sums + epsilon)
    betas.append(beta)
    last = (w_own / beta[:, None, None, None]) * norm[:, None, None, None]
    last = lax.all_to_all(last, "trait", split_axis=1, concat_axis=0, tiled=True)
    scalars = jnp.concatenate([jnp.stack(alphas, axis=1), jnp.stack(betas, axis=1)], axis=1)
    scalars = lax.all_gather(scalars, "trait", axis=0, tiled=True)
    return scalars[:, :iters], scalars[:, iters:], last


def solution(mesh):
    in_specs = (P(None, "trait", "tile", None), P("tile", None), P("tile", None), P())
    out_specs = (P(), P(), P(None, "trait", "tile", None))
    return jax.shard_map(shards, mesh=mesh, in_specs=in_specs, out_specs=out_specs, check_vma=False)
```

```python
import jax
import jax.numpy as jnp
from jax import lax
from jax.sharding import PartitionSpec as P


along_cols = 0.25
along_rows = 0.15
cross_term = 0.1
epsilon = 1e-06

HALO = 6


def nine_valid(x, kappa_rows):
    padded = jnp.pad(x, [(0, 0)] * (x.ndim - 1) + [(1, 1)])
    center = padded[..., 1:-1, 1:-1]
    sideways = padded[..., 1:-1, :-2] + padded[..., 1:-1, 2:]
    vertical = padded[..., :-2, 1:-1] + padded[..., 2:, 1:-1]
    diag_main = padded[..., 2:, 2:] + padded[..., :-2, :-2]
    diag_anti = padded[..., 2:, :-2] + padded[..., :-2, 2:]
    return (
        (kappa_rows + 2.0 * along_cols + 2.0 * along_rows) * center
        - along_cols * sideways
        - along_rows * vertical
        - 0.5 * cross_term * (diag_main - diag_anti)
    )


def gather_rows(v, axis):
    n = lax.axis_size(axis)
    return lax.all_to_all(jnp.concatenate([v] * n, axis=0), axis, 0, 0, tiled=True)


def tile_sum(v):
    n = lax.axis_size("tile")
    g = gather_rows(v, "tile").reshape((n,) + v.shape)
    return jnp.sum(g, axis=0)


def halo_rows(block, width):
    n = lax.axis_size("tile")
    dim = block.ndim - 2
    rows = block.shape[dim]
    assert rows >= width
    forward = [(i, i + 1) for i in range(n - 1)]
    backward = [(i + 1, i) for i in range(n - 1)]
    low = lax.ppermute(lax.slice_in_dim(block, rows - width, rows, axis=dim), "tile", forward)
    high = lax.ppermute(lax.slice_in_dim(block, 0, width, axis=dim), "tile", backward)
    return jnp.concatenate([low, block, high], axis=dim)


def shards(probe_signs, land_mask, kappa_sq, trait_covariance):
    rows = land_mask.shape[0]
    h = HALO
    signed = (land_mask[None, None] * (2 * probe_signs - 1)).astype(jnp.bfloat16)
    exchanged = lax.all_to_all(signed, "trait", split_axis=0, concat_axis=1, tiled=True)
    field_ext = halo_rows(exchanged, h).astype(jnp.float32)
    kappa_ext = halo_rows(kappa_sq, h)
    land_ext = field_ext[0, 0] * field_ext[0, 0]
    variances = jnp.diagonal(trait_covariance)
    z = field_ext * variances[None, :, None, None]

    def apply_a(x, off):
        r = x.shape[2]
        mixed = jnp.einsum("ts,psrc->ptrc", trait_covariance, x, precision=lax.Precision.HIGHEST)
        first = land_ext[off + 1 : off + r - 1] * nine_valid(mixed, kappa_ext[off + 1 : off + r - 1])
        return land_ext[off + 2 : off + r - 2] * nine_valid(first, kappa_ext[off + 2 : off + r - 2])

    def own(x, off):
        return x[:, :, h - off : h - off + rows]

    def dot(a, b, off):
        return jnp.sum(own(a, off) * own(b, off), axis=(1, 2, 3))

    def crop(x, k):
        return x[:, :, k : x.shape[2] - k]

    az = apply_a(z, 0)
    z2 = crop(z, 2)
    sums = tile_sum(jnp.stack([dot(z2, z2, 2), dot(az, z2, 2)], axis=-1))
    norm = jnp.sqrt(sums[:, 0] + epsilon)
    alpha = sums[:, 1] / (norm * norm)
    q = z2 / norm[:, None, None, None]
    v = az / norm[:, None, None, None]
    w = v - alpha[:, None, None, None] * q
    off = 2
    alphas = [alpha]
    betas = []
    iters = 3
    for step in range(1, iters):
        aw = apply_a(w, off)
        w2 = crop(w, 2)
        q2 = crop(q, 2)
        off += 2
        sums = tile_sum(
            jnp.stack([dot(w2, w2, off), dot(aw, w2, off), dot(q2, w2, off)], axis=-1)
        )
        beta = jnp.sqrt(sums[:, 0] + epsilon)
        alpha = sums[:, 1] / (beta * beta) - sums[:, 2]
        q_next = w2 / beta[:, None, None, None]
        v = aw / beta[:, None, None, None] - beta[:, None, None, None] * q2
        w = v - alpha[:, None, None, None] * q_next
        q = q_next
        betas.append(beta)
        alphas.append(alpha)
    w_own = own(w, off)
    w_back = lax.all_to_all(w_own, "trait", split_axis=1, concat_axis=0, tiled=True)
    sums = tile_sum(jnp.sum(w_own * w_own, axis=(1, 2, 3))[:, None])
    scalars = jnp.concatenate(
        [jnp.stack(alphas, axis=1), jnp.stack(betas, axis=1), sums, norm[:, None]], axis=1
    )
    scalars = gather_rows(scalars, "trait")
    beta = jnp.sqrt(scalars[:, 2 * iters - 1] + epsilon)
    norm_all = scalars[:, 2 * iters]
    last = (w_back / beta[:, None, None, None]) * norm_all[:, None, None, None]
    betas_all = jnp.concatenate([scalars[:, iters : 2 * iters - 1], beta[:, None]], axis=1)
    return scalars[:, :iters], betas_all, last


def solution(mesh):
    in_specs = (P(None, "trait", "tile", None), P("tile", None), P("tile", None), P())
    out_specs = (P(), P(), P(None, "trait", "tile", None))
    return jax.shard_map(shards, mesh=mesh, in_specs=in_specs, out_specs=out_specs, check_vma=False)
```

```python
import jax
import jax.numpy as jnp
from jax import lax
from jax.sharding import PartitionSpec as P


along_cols = 0.25
along_rows = 0.15
cross_term = 0.1
epsilon = 1e-06

HALO = 6


def nine_valid(x, kappa_rows):
    padded = jnp.pad(x, [(0, 0)] * (x.ndim - 1) + [(1, 1)])
    center = padded[..., 1:-1, 1:-1]
    sideways = padded[..., 1:-1, :-2] + padded[..., 1:-1, 2:]
    vertical = padded[..., :-2, 1:-1] + padded[..., 2:, 1:-1]
    diag_main = padded[..., 2:, 2:] + padded[..., :-2, :-2]
    diag_anti = padded[..., 2:, :-2] + padded[..., :-2, 2:]
    return (
        (kappa_rows + 2.0 * along_cols + 2.0 * along_rows) * center
        - along_cols * sideways
        - along_rows * vertical
        - 0.5 * cross_term * (diag_main - diag_anti)
    )


def gather_rows(v, axis):
    n = lax.axis_size(axis)
    return lax.all_to_all(jnp.concatenate([v] * n, axis=0), axis, 0, 0, tiled=True)


def tile_sum(v):
    n = lax.axis_size("tile")
    g = gather_rows(v, "tile").reshape((n,) + v.shape)
    return jnp.sum(g, axis=0)


def butterfly_sum(v, axis):
    n = lax.axis_size(axis)
    if n & (n - 1):
        return lax.psum(v, axis)
    s = 1
    while s < n:
        v = v + lax.ppermute(v, axis, [(i, i ^ s) for i in range(n)])
        s *= 2
    return v


def halo_rows(block, width):
    n = lax.axis_size("tile")
    dim = block.ndim - 2
    rows = block.shape[dim]
    assert rows >= width
    forward = [(i, i + 1) for i in range(n - 1)]
    backward = [(i + 1, i) for i in range(n - 1)]
    low = lax.ppermute(lax.slice_in_dim(block, rows - width, rows, axis=dim), "tile", forward)
    high = lax.ppermute(lax.slice_in_dim(block, 0, width, axis=dim), "tile", backward)
    return jnp.concatenate([low, block, high], axis=dim)


def shards(probe_signs, land_mask, kappa_sq, trait_covariance):
    rows = land_mask.shape[0]
    h = HALO
    signed = (land_mask[None, None] * (2 * probe_signs - 1)).astype(jnp.bfloat16)
    exchanged = lax.all_to_all(signed, "trait", split_axis=0, concat_axis=1, tiled=True)
    field_ext = halo_rows(exchanged, h).astype(jnp.float32)
    kappa_ext = halo_rows(kappa_sq, h)
    land_ext = field_ext[0, 0] * field_ext[0, 0]
    variances = jnp.diagonal(trait_covariance)
    z = field_ext * variances[None, :, None, None]

    def apply_a(x, off):
        r = x.shape[2]
        mixed = jnp.einsum("ts,psrc->ptrc", trait_covariance, x, precision=lax.Precision.HIGHEST)
        first = land_ext[off + 1 : off + r - 1] * nine_valid(mixed, kappa_ext[off + 1 : off + r - 1])
        return land_ext[off + 2 : off + r - 2] * nine_valid(first, kappa_ext[off + 2 : off + r - 2])

    def own(x, off):
        return x[:, :, h - off : h - off + rows]

    def dot(a, b, off):
        return jnp.sum(own(a, off) * own(b, off), axis=(1, 2, 3))

    def crop(x, k):
        return x[:, :, k : x.shape[2] - k]

    az = apply_a(z, 0)
    z2 = crop(z, 2)
    sums = tile_sum(jnp.stack([dot(z2, z2, 2), dot(az, z2, 2)], axis=-1))
    norm = jnp.sqrt(sums[:, 0] + epsilon)
    alpha = sums[:, 1] / (norm * norm)
    q = z2 / norm[:, None, None, None]
    v = az / norm[:, None, None, None]
    w = v - alpha[:, None, None, None] * q
    off = 2
    alphas = [alpha]
    betas = []
    iters = 3
    for step in range(1, iters):
        aw = apply_a(w, off)
        w2 = crop(w, 2)
        q2 = crop(q, 2)
        off += 2
        sums = tile_sum(
            jnp.stack([dot(w2, w2, off), dot(aw, w2, off), dot(q2, w2, off)], axis=-1)
        )
        beta = jnp.sqrt(sums[:, 0] + epsilon)
        alpha = sums[:, 1] / (beta * beta) - sums[:, 2]
        q_next = w2 / beta[:, None, None, None]
        v = aw / beta[:, None, None, None] - beta[:, None, None, None] * q2
        w = v - alpha[:, None, None, None] * q_next
        q = q_next
        betas.append(beta)
        alphas.append(alpha)
    w_own = own(w, off)
    w_back = lax.all_to_all(w_own, "trait", split_axis=1, concat_axis=0, tiled=True)
    partial = jnp.sum(w_own * w_own, axis=(1, 2, 3))[:, None]
    first = (lax.axis_index("tile") == 0).astype(jnp.float32)
    known = jnp.concatenate([jnp.stack(alphas, axis=1), jnp.stack(betas, axis=1)], axis=1)
    mine = jnp.concatenate([known * first, partial, norm[:, None] * first], axis=1)
    probes_local = mine.shape[0]
    n_trait = lax.axis_size("trait")
    spread = lax.dynamic_update_slice(
        jnp.zeros((probes_local * n_trait, mine.shape[1]), jnp.float32),
        mine,
        (lax.axis_index("trait") * probes_local, 0),
    )
    scalars = butterfly_sum(butterfly_sum(spread, "tile"), "trait")
    beta = jnp.sqrt(scalars[:, 2 * iters - 1] + epsilon)
    norm_all = scalars[:, 2 * iters]
    last = (w_back / beta[:, None, None, None]) * norm_all[:, None, None, None]
    betas_all = jnp.concatenate([scalars[:, iters : 2 * iters - 1], beta[:, None]], axis=1)
    return scalars[:, :iters], betas_all, last


def solution(mesh):
    in_specs = (P(None, "trait", "tile", None), P("tile", None), P("tile", None), P())
    out_specs = (P(), P(), P(None, "trait", "tile", None))
    return jax.shard_map(shards, mesh=mesh, in_specs=in_specs, out_specs=out_specs, check_vma=False)
```

```python
import jax
import jax.numpy as jnp
from jax import lax
from jax.sharding import PartitionSpec as P


along_cols = 0.25
along_rows = 0.15
cross_term = 0.1
epsilon = 1e-06

HALO = 6


def nine_valid(x, kappa_rows):
    padded = jnp.pad(x, [(0, 0)] * (x.ndim - 1) + [(1, 1)])
    center = padded[..., 1:-1, 1:-1]
    sideways = padded[..., 1:-1, :-2] + padded[..., 1:-1, 2:]
    vertical = padded[..., :-2, 1:-1] + padded[..., 2:, 1:-1]
    diag_main = padded[..., 2:, 2:] + padded[..., :-2, :-2]
    diag_anti = padded[..., 2:, :-2] + padded[..., :-2, 2:]
    return (
        (kappa_rows + 2.0 * along_cols + 2.0 * along_rows) * center
        - along_cols * sideways
        - along_rows * vertical
        - 0.5 * cross_term * (diag_main - diag_anti)
    )


def gather_rows(v, axis):
    n = lax.axis_size(axis)
    return lax.all_to_all(jnp.concatenate([v] * n, axis=0), axis, 0, 0, tiled=True)


def tile_sum(v):
    n = lax.axis_size("tile")
    g = gather_rows(v, "tile").reshape((n,) + v.shape)
    return jnp.sum(g, axis=0)


def butterfly_sum(v, axis):
    n = lax.axis_size(axis)
    if n & (n - 1):
        return lax.psum(v, axis)
    s = 1
    while s < n:
        v = v + lax.ppermute(v, axis, [(i, i ^ s) for i in range(n)])
        s *= 2
    return v


def halo_rows(block, width):
    n = lax.axis_size("tile")
    dim = block.ndim - 2
    rows = block.shape[dim]
    assert rows >= width
    forward = [(i, i + 1) for i in range(n - 1)]
    backward = [(i + 1, i) for i in range(n - 1)]
    low = lax.ppermute(lax.slice_in_dim(block, rows - width, rows, axis=dim), "tile", forward)
    high = lax.ppermute(lax.slice_in_dim(block, 0, width, axis=dim), "tile", backward)
    return jnp.concatenate([low, block, high], axis=dim)


def shards(probe_signs, land_mask, kappa_sq, trait_covariance):
    rows = land_mask.shape[0]
    h = HALO
    signed = (land_mask[None, None] * (2 * probe_signs - 1)).astype(jnp.bfloat16)
    exchanged = lax.all_to_all(signed, "trait", split_axis=0, concat_axis=1, tiled=True)
    field_ext = halo_rows(exchanged, h).astype(jnp.float32)
    kappa_ext = halo_rows(kappa_sq, h)
    land_ext = field_ext[0, 0] * field_ext[0, 0]
    variances = jnp.diagonal(trait_covariance)
    z = field_ext * variances[None, :, None, None]

    def apply_a(x, off):
        r = x.shape[2]
        mixed = jnp.einsum("ts,psrc->ptrc", trait_covariance, x, precision=lax.Precision.HIGHEST)
        first = land_ext[off + 1 : off + r - 1] * nine_valid(mixed, kappa_ext[off + 1 : off + r - 1])
        return land_ext[off + 2 : off + r - 2] * nine_valid(first, kappa_ext[off + 2 : off + r - 2])

    def own(x, off):
        return x[:, :, h - off : h - off + rows]

    def dot(a, b, off):
        return jnp.sum(own(a, off) * own(b, off), axis=(1, 2, 3))

    def crop(x, k):
        return x[:, :, k : x.shape[2] - k]

    def reduce_tile(parts):
        return butterfly_sum(lax.optimization_barrier(jnp.stack(parts, axis=-1)), "tile")

    az = apply_a(z, 0)
    z2 = crop(z, 2)
    sums = reduce_tile([dot(z2, z2, 2), dot(az, z2, 2)])
    aaz = apply_a(az, 2)
    norm = jnp.sqrt(sums[:, 0] + epsilon)
    alpha = sums[:, 1] / (norm * norm)
    q = z2 / norm[:, None, None, None]
    aq = az / norm[:, None, None, None]
    w = aq - alpha[:, None, None, None] * q
    aw = aaz / norm[:, None, None, None] - alpha[:, None, None, None] * crop(aq, 2)
    aq = crop(aq, 2)
    q = crop(q, 2)
    w = crop(w, 2)
    off = 4
    alphas = [alpha]
    betas = []
    iters = 3
    for step in range(1, iters):
        sums = reduce_tile([dot(w, w, off), dot(aw, w, off), dot(q, w, off)])
        last_step = step == iters - 1
        if not last_step:
            aaw = apply_a(aw, off)
        beta = jnp.sqrt(sums[:, 0] + epsilon)
        alpha = sums[:, 1] / (beta * beta) - sums[:, 2]
        q_next = w / beta[:, None, None, None]
        w_next = aw / beta[:, None, None, None] - beta[:, None, None, None] * q - alpha[:, None, None, None] * q_next
        if not last_step:
            aw_next = (
                aaw / beta[:, None, None, None]
                - beta[:, None, None, None] * crop(aq, 2)
                - alpha[:, None, None, None] * crop(aw, 2) / beta[:, None, None, None]
            )
            aq = crop(aw, 2) / beta[:, None, None, None]
            q = crop(q_next, 2)
            w = crop(w_next, 2)
            aw = aw_next
            off += 2
        else:
            q = q_next
            w = w_next
        betas.append(beta)
        alphas.append(alpha)
    w_own = own(w, off)
    w_back = lax.all_to_all(w_own, "trait", split_axis=1, concat_axis=0, tiled=True)
    partial = jnp.sum(w_own * w_own, axis=(1, 2, 3))[:, None]
    first = (lax.axis_index("tile") == 0).astype(jnp.float32)
    known = jnp.concatenate([jnp.stack(alphas, axis=1), jnp.stack(betas, axis=1)], axis=1)
    mine = jnp.concatenate([known * first, partial, norm[:, None] * first], axis=1)
    probes_local = mine.shape[0]
    n_trait = lax.axis_size("trait")
    spread = lax.dynamic_update_slice(
        jnp.zeros((probes_local * n_trait, mine.shape[1]), jnp.float32),
        mine,
        (lax.axis_index("trait") * probes_local, 0),
    )
    scalars = butterfly_sum(butterfly_sum(spread, "tile"), "trait")
    beta = jnp.sqrt(scalars[:, 2 * iters - 1] + epsilon)
    norm_all = scalars[:, 2 * iters]
    last = (w_back / beta[:, None, None, None]) * norm_all[:, None, None, None]
    betas_all = jnp.concatenate([scalars[:, iters : 2 * iters - 1], beta[:, None]], axis=1)
    return scalars[:, :iters], betas_all, last


def solution(mesh):
    in_specs = (P(None, "trait", "tile", None), P("tile", None), P("tile", None), P())
    out_specs = (P(), P(), P(None, "trait", "tile", None))
    return jax.shard_map(shards, mesh=mesh, in_specs=in_specs, out_specs=out_specs, check_vma=False)
```

```python
import jax
import jax.numpy as jnp
from jax import lax
from jax.sharding import PartitionSpec as P


along_cols = 0.25
along_rows = 0.15
cross_term = 0.1
epsilon = 1e-06

HALO = 6


def nine_valid(x, kappa_rows):
    padded = jnp.pad(x, [(0, 0)] * (x.ndim - 1) + [(1, 1)])
    center = padded[..., 1:-1, 1:-1]
    sideways = padded[..., 1:-1, :-2] + padded[..., 1:-1, 2:]
    vertical = padded[..., :-2, 1:-1] + padded[..., 2:, 1:-1]
    diag_main = padded[..., 2:, 2:] + padded[..., :-2, :-2]
    diag_anti = padded[..., 2:, :-2] + padded[..., :-2, 2:]
    return (
        (kappa_rows + 2.0 * along_cols + 2.0 * along_rows) * center
        - along_cols * sideways
        - along_rows * vertical
        - 0.5 * cross_term * (diag_main - diag_anti)
    )


def gather_rows(v, axis):
    n = lax.axis_size(axis)
    return lax.all_to_all(jnp.concatenate([v] * n, axis=0), axis, 0, 0, tiled=True)


def tile_sum(v):
    n = lax.axis_size("tile")
    g = gather_rows(v, "tile").reshape((n,) + v.shape)
    return jnp.sum(g, axis=0)


def butterfly_sum(v, axis):
    n = lax.axis_size(axis)
    if n & (n - 1):
        return lax.psum(v, axis)
    s = 1
    while s < n:
        v = v + lax.ppermute(v, axis, [(i, i ^ s) for i in range(n)])
        s *= 2
    return v


def halo_rows(block, width):
    n = lax.axis_size("tile")
    dim = block.ndim - 2
    rows = block.shape[dim]
    assert rows >= width
    forward = [(i, i + 1) for i in range(n - 1)]
    backward = [(i + 1, i) for i in range(n - 1)]
    low = lax.ppermute(lax.slice_in_dim(block, rows - width, rows, axis=dim), "tile", forward)
    high = lax.ppermute(lax.slice_in_dim(block, 0, width, axis=dim), "tile", backward)
    return jnp.concatenate([low, block, high], axis=dim)


def shards(probe_signs, land_mask, kappa_sq, trait_covariance):
    rows = land_mask.shape[0]
    h = HALO
    signed = (land_mask[None, None] * (2 * probe_signs - 1)).astype(jnp.bfloat16)
    exchanged = lax.all_to_all(signed, "trait", split_axis=0, concat_axis=1, tiled=True)
    field_ext = halo_rows(exchanged, h).astype(jnp.float32)
    kappa_ext = halo_rows(kappa_sq, h)
    land_ext = field_ext[0, 0] * field_ext[0, 0]
    variances = jnp.diagonal(trait_covariance)
    z = field_ext * variances[None, :, None, None]

    def apply_a(x, off):
        r = x.shape[2]
        mixed = jnp.einsum("ts,psrc->ptrc", trait_covariance, x, precision=lax.Precision.HIGHEST)
        first = land_ext[off + 1 : off + r - 1] * nine_valid(mixed, kappa_ext[off + 1 : off + r - 1])
        return land_ext[off + 2 : off + r - 2] * nine_valid(first, kappa_ext[off + 2 : off + r - 2])

    def own(x, off):
        return x[:, :, h - off : h - off + rows]

    def dot(a, b, off):
        return jnp.sum(own(a, off) * own(b, off), axis=(1, 2, 3))

    def crop(x, k):
        return x[:, :, k : x.shape[2] - k]

    def reduce_tile(pairs, off):
        prods = jnp.stack([own(a, off) * own(b, off) for a, b in pairs], axis=-1)
        return butterfly_sum(jnp.sum(prods, axis=(1, 2, 3)), "tile")

    az = apply_a(z, 0)
    z2 = crop(z, 2)
    sums = reduce_tile([(z2, z2), (az, z2)], 2)
    aaz = apply_a(az, 2)
    norm = jnp.sqrt(sums[:, 0] + epsilon)
    alpha = sums[:, 1] / (norm * norm)
    q = z2 / norm[:, None, None, None]
    aq = az / norm[:, None, None, None]
    w = aq - alpha[:, None, None, None] * q
    aw = aaz / norm[:, None, None, None] - alpha[:, None, None, None] * crop(aq, 2)
    aq = crop(aq, 2)
    q = crop(q, 2)
    w = crop(w, 2)
    off = 4
    alphas = [alpha]
    betas = []
    iters = 3
    for step in range(1, iters):
        sums = reduce_tile([(w, w), (aw, w), (q, w)], off)
        last_step = step == iters - 1
        if not last_step:
            aaw = apply_a(aw, off)
        beta = jnp.sqrt(sums[:, 0] + epsilon)
        alpha = sums[:, 1] / (beta * beta) - sums[:, 2]
        q_next = w / beta[:, None, None, None]
        w_next = aw / beta[:, None, None, None] - beta[:, None, None, None] * q - alpha[:, None, None, None] * q_next
        if not last_step:
            aw_next = (
                aaw / beta[:, None, None, None]
                - beta[:, None, None, None] * crop(aq, 2)
                - alpha[:, None, None, None] * crop(aw, 2) / beta[:, None, None, None]
            )
            aq = crop(aw, 2) / beta[:, None, None, None]
            q = crop(q_next, 2)
            w = crop(w_next, 2)
            aw = aw_next
            off += 2
        else:
            q = q_next
            w = w_next
        betas.append(beta)
        alphas.append(alpha)
    w_own = own(w, off)
    w_back = lax.all_to_all(w_own, "trait", split_axis=1, concat_axis=0, tiled=True)
    partial = jnp.sum(w_own * w_own, axis=(1, 2, 3))[:, None]
    first = (lax.axis_index("tile") == 0).astype(jnp.float32)
    known = jnp.concatenate([jnp.stack(alphas, axis=1), jnp.stack(betas, axis=1)], axis=1)
    mine = jnp.concatenate([known * first, partial, norm[:, None] * first], axis=1)
    probes_local = mine.shape[0]
    n_trait = lax.axis_size("trait")
    spread = lax.dynamic_update_slice(
        jnp.zeros((probes_local * n_trait, mine.shape[1]), jnp.float32),
        mine,
        (lax.axis_index("trait") * probes_local, 0),
    )
    scalars = butterfly_sum(butterfly_sum(spread, "tile"), "trait")
    beta = jnp.sqrt(scalars[:, 2 * iters - 1] + epsilon)
    norm_all = scalars[:, 2 * iters]
    last = (w_back / beta[:, None, None, None]) * norm_all[:, None, None, None]
    betas_all = jnp.concatenate([scalars[:, iters : 2 * iters - 1], beta[:, None]], axis=1)
    return scalars[:, :iters], betas_all, last


def solution(mesh):
    in_specs = (P(None, "trait", "tile", None), P("tile", None), P("tile", None), P())
    out_specs = (P(), P(), P(None, "trait", "tile", None))
    return jax.shard_map(shards, mesh=mesh, in_specs=in_specs, out_specs=out_specs, check_vma=False)
```

```python
import jax
import jax.numpy as jnp
from jax import lax
from jax.sharding import PartitionSpec as P


along_cols = 0.25
along_rows = 0.15
cross_term = 0.1
epsilon = 1e-06

HALO = 6


def nine_valid(x, kappa_rows):
    padded = jnp.pad(x, [(0, 0)] * (x.ndim - 1) + [(1, 1)])
    center = padded[..., 1:-1, 1:-1]
    sideways = padded[..., 1:-1, :-2] + padded[..., 1:-1, 2:]
    vertical = padded[..., :-2, 1:-1] + padded[..., 2:, 1:-1]
    diag_main = padded[..., 2:, 2:] + padded[..., :-2, :-2]
    diag_anti = padded[..., 2:, :-2] + padded[..., :-2, 2:]
    return (
        (kappa_rows + 2.0 * along_cols + 2.0 * along_rows) * center
        - along_cols * sideways
        - along_rows * vertical
        - 0.5 * cross_term * (diag_main - diag_anti)
    )


def gather_rows(v, axis):
    n = lax.axis_size(axis)
    return lax.all_to_all(jnp.concatenate([v] * n, axis=0), axis, 0, 0, tiled=True)


def tile_sum(v):
    n = lax.axis_size("tile")
    g = gather_rows(v, "tile").reshape((n,) + v.shape)
    return jnp.sum(g, axis=0)


def butterfly_sum(v, axis):
    n = lax.axis_size(axis)
    if n & (n - 1):
        return lax.psum(v, axis)
    s = 1
    while s < n:
        v = v + lax.ppermute(v, axis, [(i, i ^ s) for i in range(n)])
        s *= 2
    return v


def halo_rows(block, width):
    n = lax.axis_size("tile")
    dim = block.ndim - 2
    rows = block.shape[dim]
    assert rows >= width
    forward = [(i, i + 1) for i in range(n - 1)]
    backward = [(i + 1, i) for i in range(n - 1)]
    low = lax.ppermute(lax.slice_in_dim(block, rows - width, rows, axis=dim), "tile", forward)
    high = lax.ppermute(lax.slice_in_dim(block, 0, width, axis=dim), "tile", backward)
    return jnp.concatenate([low, block, high], axis=dim)


def shards(probe_signs, land_mask, kappa_sq, trait_covariance):
    rows = land_mask.shape[0]
    h = HALO
    signed = (land_mask[None, None] * (2 * probe_signs - 1)).astype(jnp.bfloat16)
    exchanged = lax.all_to_all(signed, "trait", split_axis=0, concat_axis=1, tiled=True)
    field_ext = halo_rows(exchanged, h).astype(jnp.float32)
    kappa_ext = halo_rows(kappa_sq, h)
    land_ext = field_ext[0, 0] * field_ext[0, 0]
    variances = jnp.diagonal(trait_covariance)
    z = field_ext * variances[None, :, None, None]

    def apply_a(x, off):
        r = x.shape[2]
        mixed = jnp.einsum("ts,psrc->ptrc", trait_covariance, x, precision=lax.Precision.HIGH)
        first = land_ext[off + 1 : off + r - 1] * nine_valid(mixed, kappa_ext[off + 1 : off + r - 1])
        return land_ext[off + 2 : off + r - 2] * nine_valid(first, kappa_ext[off + 2 : off + r - 2])

    def own(x, off):
        return x[:, :, h - off : h - off + rows]

    def dot(a, b, off):
        return jnp.sum(own(a, off) * own(b, off), axis=(1, 2, 3))

    def crop(x, k):
        return x[:, :, k : x.shape[2] - k]

    def reduce_tile(pairs, off):
        prods = jnp.stack([own(a, off) * own(b, off) for a, b in pairs], axis=-1)
        return butterfly_sum(jnp.sum(prods, axis=(1, 2, 3)), "tile")

    az = apply_a(z, 0)
    z2 = crop(z, 2)
    sums = reduce_tile([(z2, z2), (az, z2)], 2)
    aaz = apply_a(az, 2)
    norm = jnp.sqrt(sums[:, 0] + epsilon)
    alpha = sums[:, 1] / (norm * norm)
    q = z2 / norm[:, None, None, None]
    aq = az / norm[:, None, None, None]
    w = aq - alpha[:, None, None, None] * q
    aw = aaz / norm[:, None, None, None] - alpha[:, None, None, None] * crop(aq, 2)
    aq = crop(aq, 2)
    q = crop(q, 2)
    w = crop(w, 2)
    off = 4
    alphas = [alpha]
    betas = []
    iters = 3
    for step in range(1, iters):
        sums = reduce_tile([(w, w), (aw, w), (q, w)], off)
        last_step = step == iters - 1
        if not last_step:
            aaw = apply_a(aw, off)
        beta = jnp.sqrt(sums[:, 0] + epsilon)
        alpha = sums[:, 1] / (beta * beta) - sums[:, 2]
        q_next = w / beta[:, None, None, None]
        w_next = aw / beta[:, None, None, None] - beta[:, None, None, None] * q - alpha[:, None, None, None] * q_next
        if not last_step:
            aw_next = (
                aaw / beta[:, None, None, None]
                - beta[:, None, None, None] * crop(aq, 2)
                - alpha[:, None, None, None] * crop(aw, 2) / beta[:, None, None, None]
            )
            aq = crop(aw, 2) / beta[:, None, None, None]
            q = crop(q_next, 2)
            w = crop(w_next, 2)
            aw = aw_next
            off += 2
        else:
            q = q_next
            w = w_next
        betas.append(beta)
        alphas.append(alpha)
    w_own = own(w, off)
    w_back = lax.all_to_all(w_own, "trait", split_axis=1, concat_axis=0, tiled=True)
    partial = jnp.sum(w_own * w_own, axis=(1, 2, 3))[:, None]
    first = (lax.axis_index("tile") == 0).astype(jnp.float32)
    known = jnp.concatenate([jnp.stack(alphas, axis=1), jnp.stack(betas, axis=1)], axis=1)
    mine = jnp.concatenate([known * first, partial, norm[:, None] * first], axis=1)
    probes_local = mine.shape[0]
    n_trait = lax.axis_size("trait")
    spread = lax.dynamic_update_slice(
        jnp.zeros((probes_local * n_trait, mine.shape[1]), jnp.float32),
        mine,
        (lax.axis_index("trait") * probes_local, 0),
    )
    scalars = butterfly_sum(butterfly_sum(spread, "tile"), "trait")
    beta = jnp.sqrt(scalars[:, 2 * iters - 1] + epsilon)
    norm_all = scalars[:, 2 * iters]
    last = (w_back / beta[:, None, None, None]) * norm_all[:, None, None, None]
    betas_all = jnp.concatenate([scalars[:, iters : 2 * iters - 1], beta[:, None]], axis=1)
    return scalars[:, :iters], betas_all, last


def solution(mesh):
    in_specs = (P(None, "trait", "tile", None), P("tile", None), P("tile", None), P())
    out_specs = (P(), P(), P(None, "trait", "tile", None))
    return jax.shard_map(shards, mesh=mesh, in_specs=in_specs, out_specs=out_specs, check_vma=False)
```

```python
import jax
import jax.numpy as jnp
from jax import lax
from jax.sharding import PartitionSpec as P


along_cols = 0.25
along_rows = 0.15
cross_term = 0.1
epsilon = 1e-06

HALO = 6


def nine_valid(x, kappa_rows):
    padded = jnp.pad(x, [(0, 0)] * (x.ndim - 1) + [(1, 1)])
    center = padded[..., 1:-1, 1:-1]
    sideways = padded[..., 1:-1, :-2] + padded[..., 1:-1, 2:]
    vertical = padded[..., :-2, 1:-1] + padded[..., 2:, 1:-1]
    diag_main = padded[..., 2:, 2:] + padded[..., :-2, :-2]
    diag_anti = padded[..., 2:, :-2] + padded[..., :-2, 2:]
    return (
        (kappa_rows + 2.0 * along_cols + 2.0 * along_rows) * center
        - along_cols * sideways
        - along_rows * vertical
        - 0.5 * cross_term * (diag_main - diag_anti)
    )


def gather_rows(v, axis):
    n = lax.axis_size(axis)
    return lax.all_to_all(jnp.concatenate([v] * n, axis=0), axis, 0, 0, tiled=True)


def tile_sum(v):
    n = lax.axis_size("tile")
    g = gather_rows(v, "tile").reshape((n,) + v.shape)
    return jnp.sum(g, axis=0)


def butterfly_sum(v, axis, work=()):
    n = lax.axis_size(axis)
    carry = None
    if n & (n - 1):
        for stage in work:
            carry = stage(carry)
        return lax.psum(v, axis), carry
    s = 1
    r = 0
    while s < n:
        got = lax.ppermute(v, axis, [(i, i ^ s) for i in range(n)])
        if r < len(work):
            carry = work[r](carry)
            v, carry = lax.optimization_barrier((v + got, carry))
        else:
            v = v + got
        s *= 2
        r += 1
    for stage in work[r:]:
        carry = stage(carry)
    return v, carry


def halo_rows(block, width):
    n = lax.axis_size("tile")
    dim = block.ndim - 2
    rows = block.shape[dim]
    assert rows >= width
    forward = [(i, i + 1) for i in range(n - 1)]
    backward = [(i + 1, i) for i in range(n - 1)]
    low = lax.ppermute(lax.slice_in_dim(block, rows - width, rows, axis=dim), "tile", forward)
    high = lax.ppermute(lax.slice_in_dim(block, 0, width, axis=dim), "tile", backward)
    return jnp.concatenate([low, block, high], axis=dim)


def shards(probe_signs, land_mask, kappa_sq, trait_covariance):
    rows = land_mask.shape[0]
    h = HALO
    signed = (land_mask[None, None] * (2 * probe_signs - 1)).astype(jnp.bfloat16)
    exchanged = lax.all_to_all(signed, "trait", split_axis=0, concat_axis=1, tiled=True)
    field_ext = halo_rows(exchanged, h).astype(jnp.float32)
    kappa_ext = halo_rows(kappa_sq, h)
    land_ext = field_ext[0, 0] * field_ext[0, 0]
    variances = jnp.diagonal(trait_covariance)
    z = field_ext * variances[None, :, None, None]

    def apply_half(x, off, mix):
        r = x.shape[2]
        if mix:
            x = jnp.einsum("ts,psrc->ptrc", trait_covariance, x, precision=lax.Precision.HIGHEST)
        return land_ext[off + 1 : off + r - 1] * nine_valid(x, kappa_ext[off + 1 : off + r - 1])

    def apply_a(x, off):
        return apply_half(apply_half(x, off, True), off + 1, False)

    def a_stages(x, off):
        return (lambda _: apply_half(x, off, True), lambda first: apply_half(first, off + 1, False))

    def own(x, off):
        return x[:, :, h - off : h - off + rows]

    def dot(a, b, off):
        return jnp.sum(own(a, off) * own(b, off), axis=(1, 2, 3))

    def crop(x, k):
        return x[:, :, k : x.shape[2] - k]

    def reduce_tile(pairs, off, work=()):
        prods = jnp.stack([own(a, off) * own(b, off) for a, b in pairs], axis=-1)
        return butterfly_sum(jnp.sum(prods, axis=(1, 2, 3)), "tile", work)

    az = apply_a(z, 0)
    z2 = crop(z, 2)
    sums, aaz = reduce_tile([(z2, z2), (az, z2)], 2, a_stages(az, 2))
    norm = jnp.sqrt(sums[:, 0] + epsilon)
    alpha = sums[:, 1] / (norm * norm)
    q = z2 / norm[:, None, None, None]
    aq = az / norm[:, None, None, None]
    w = aq - alpha[:, None, None, None] * q
    aw = aaz / norm[:, None, None, None] - alpha[:, None, None, None] * crop(aq, 2)
    aq = crop(aq, 2)
    q = crop(q, 2)
    w = crop(w, 2)
    off = 4
    alphas = [alpha]
    betas = []
    iters = 3
    for step in range(1, iters):
        last_step = step == iters - 1
        sums, aaw = reduce_tile([(w, w), (aw, w), (q, w)], off, () if last_step else a_stages(aw, off))
        beta = jnp.sqrt(sums[:, 0] + epsilon)
        alpha = sums[:, 1] / (beta * beta) - sums[:, 2]
        q_next = w / beta[:, None, None, None]
        w_next = aw / beta[:, None, None, None] - beta[:, None, None, None] * q - alpha[:, None, None, None] * q_next
        if not last_step:
            aw_next = (
                aaw / beta[:, None, None, None]
                - beta[:, None, None, None] * crop(aq, 2)
                - alpha[:, None, None, None] * crop(aw, 2) / beta[:, None, None, None]
            )
            aq = crop(aw, 2) / beta[:, None, None, None]
            q = crop(q_next, 2)
            w = crop(w_next, 2)
            aw = aw_next
            off += 2
        else:
            q = q_next
            w = w_next
        betas.append(beta)
        alphas.append(alpha)
    w_own = own(w, off)
    w_back = lax.all_to_all(w_own, "trait", split_axis=1, concat_axis=0, tiled=True)
    partial = jnp.sum(w_own * w_own, axis=(1, 2, 3))[:, None]
    first = (lax.axis_index("tile") == 0).astype(jnp.float32)
    known = jnp.concatenate([jnp.stack(alphas, axis=1), jnp.stack(betas, axis=1)], axis=1)
    mine = jnp.concatenate([known * first, partial, norm[:, None] * first], axis=1)
    probes_local = mine.shape[0]
    n_trait = lax.axis_size("trait")
    spread = lax.dynamic_update_slice(
        jnp.zeros((probes_local * n_trait, mine.shape[1]), jnp.float32),
        mine,
        (lax.axis_index("trait") * probes_local, 0),
    )
    scalars = butterfly_sum(butterfly_sum(spread, "tile")[0], "trait")[0]
    beta = jnp.sqrt(scalars[:, 2 * iters - 1] + epsilon)
    norm_all = scalars[:, 2 * iters]
    last = (w_back / beta[:, None, None, None]) * norm_all[:, None, None, None]
    betas_all = jnp.concatenate([scalars[:, iters : 2 * iters - 1], beta[:, None]], axis=1)
    return scalars[:, :iters], betas_all, last


def solution(mesh):
    in_specs = (P(None, "trait", "tile", None), P("tile", None), P("tile", None), P())
    out_specs = (P(), P(), P(None, "trait", "tile", None))
    return jax.shard_map(shards, mesh=mesh, in_specs=in_specs, out_specs=out_specs, check_vma=False)
```

```python
import jax
import jax.numpy as jnp
from jax import lax
from jax.sharding import PartitionSpec as P


along_cols = 0.25
along_rows = 0.15
cross_term = 0.1
epsilon = 1e-06

HALO = 6


def nine_valid(x, kappa_rows):
    padded = jnp.pad(x, [(0, 0)] * (x.ndim - 1) + [(1, 1)])
    center = padded[..., 1:-1, 1:-1]
    sideways = padded[..., 1:-1, :-2] + padded[..., 1:-1, 2:]
    vertical = padded[..., :-2, 1:-1] + padded[..., 2:, 1:-1]
    diag_main = padded[..., 2:, 2:] + padded[..., :-2, :-2]
    diag_anti = padded[..., 2:, :-2] + padded[..., :-2, 2:]
    return (
        (kappa_rows + 2.0 * along_cols + 2.0 * along_rows) * center
        - along_cols * sideways
        - along_rows * vertical
        - 0.5 * cross_term * (diag_main - diag_anti)
    )


def gather_rows(v, axis):
    n = lax.axis_size(axis)
    return lax.all_to_all(jnp.concatenate([v] * n, axis=0), axis, 0, 0, tiled=True)


def tile_sum(v):
    n = lax.axis_size("tile")
    g = gather_rows(v, "tile").reshape((n,) + v.shape)
    return jnp.sum(g, axis=0)


def butterfly_sum(v, axis, work=()):
    n = lax.axis_size(axis)
    carry = None
    if n & (n - 1):
        for stage in work:
            carry = stage(carry)
        return lax.psum(v, axis), carry
    s = 1
    r = 0
    while s < n:
        got = lax.ppermute(v, axis, [(i, i ^ s) for i in range(n)])
        if r < len(work):
            carry = work[r](carry)
            v, carry = lax.optimization_barrier((v + got, carry))
        else:
            v = v + got
        s *= 2
        r += 1
    for stage in work[r:]:
        carry = stage(carry)
    return v, carry


def halo_rows(block, width):
    n = lax.axis_size("tile")
    dim = block.ndim - 2
    rows = block.shape[dim]
    assert rows >= width
    forward = [(i, i + 1) for i in range(n - 1)]
    backward = [(i + 1, i) for i in range(n - 1)]
    low = lax.ppermute(lax.slice_in_dim(block, rows - width, rows, axis=dim), "tile", forward)
    high = lax.ppermute(lax.slice_in_dim(block, 0, width, axis=dim), "tile", backward)
    return jnp.concatenate([low, block, high], axis=dim)


def shards(probe_signs, land_mask, kappa_sq, trait_covariance):
    rows = land_mask.shape[0]
    h = HALO
    signed = (land_mask[None, None] * (2 * probe_signs - 1)).astype(jnp.bfloat16)
    exchanged = lax.all_to_all(signed, "trait", split_axis=0, concat_axis=1, tiled=True)
    field_ext = halo_rows(exchanged, h).astype(jnp.float32)
    kappa_ext = halo_rows(kappa_sq, h)
    land_ext = field_ext[0, 0] * field_ext[0, 0]
    variances = jnp.diagonal(trait_covariance)
    z = field_ext * variances[None, :, None, None]

    def mix(x):
        return jnp.einsum("ts,psrc->ptrc", trait_covariance, x, precision=lax.Precision.HIGHEST)

    def stencil(x, off):
        r = x.shape[2]
        return land_ext[off + 1 : off + r - 1] * nine_valid(x, kappa_ext[off + 1 : off + r - 1])

    def apply_a(x, off):
        return mix(stencil(stencil(x, off), off + 1))

    def a_stages(x, off):
        return (lambda _: stencil(x, off), lambda first: mix(stencil(first, off + 1)))

    def own(x, off):
        return x[:, :, h - off : h - off + rows]

    def dot(a, b, off):
        return jnp.sum(own(a, off) * own(b, off), axis=(1, 2, 3))

    def crop(x, k):
        return x[:, :, k : x.shape[2] - k]

    def reduce_tile(pairs, off, work=()):
        prods = jnp.stack([own(a, off) * own(b, off) for a, b in pairs], axis=-1)
        return butterfly_sum(jnp.sum(prods, axis=(1, 2, 3)), "tile", work)

    az = apply_a(z, 0)
    z2 = crop(z, 2)
    sums, aaz = reduce_tile([(z2, z2), (az, z2)], 2, a_stages(az, 2))
    norm = jnp.sqrt(sums[:, 0] + epsilon)
    alpha = sums[:, 1] / (norm * norm)
    q = z2 / norm[:, None, None, None]
    aq = az / norm[:, None, None, None]
    w = aq - alpha[:, None, None, None] * q
    aw = aaz / norm[:, None, None, None] - alpha[:, None, None, None] * crop(aq, 2)
    aq = crop(aq, 2)
    q = crop(q, 2)
    w = crop(w, 2)
    off = 4
    alphas = [alpha]
    betas = []
    iters = 3
    for step in range(1, iters):
        last_step = step == iters - 1
        sums, aaw = reduce_tile([(w, w), (aw, w), (q, w)], off, () if last_step else a_stages(aw, off))
        beta = jnp.sqrt(sums[:, 0] + epsilon)
        alpha = sums[:, 1] / (beta * beta) - sums[:, 2]
        q_next = w / beta[:, None, None, None]
        w_next = aw / beta[:, None, None, None] - beta[:, None, None, None] * q - alpha[:, None, None, None] * q_next
        if not last_step:
            aw_next = (
                aaw / beta[:, None, None, None]
                - beta[:, None, None, None] * crop(aq, 2)
                - alpha[:, None, None, None] * crop(aw, 2) / beta[:, None, None, None]
            )
            aq = crop(aw, 2) / beta[:, None, None, None]
            q = crop(q_next, 2)
            w = crop(w_next, 2)
            aw = aw_next
            off += 2
        else:
            q = q_next
            w = w_next
        betas.append(beta)
        alphas.append(alpha)
    w_own = own(w, off)
    w_back = lax.all_to_all(w_own, "trait", split_axis=1, concat_axis=0, tiled=True)
    partial = jnp.sum(w_own * w_own, axis=(1, 2, 3))[:, None]
    first = (lax.axis_index("tile") == 0).astype(jnp.float32)
    known = jnp.concatenate([jnp.stack(alphas, axis=1), jnp.stack(betas, axis=1)], axis=1)
    mine = jnp.concatenate([known * first, partial, norm[:, None] * first], axis=1)
    probes_local = mine.shape[0]
    n_trait = lax.axis_size("trait")
    spread = lax.dynamic_update_slice(
        jnp.zeros((probes_local * n_trait, mine.shape[1]), jnp.float32),
        mine,
        (lax.axis_index("trait") * probes_local, 0),
    )
    scalars = butterfly_sum(butterfly_sum(spread, "tile")[0], "trait")[0]
    beta = jnp.sqrt(scalars[:, 2 * iters - 1] + epsilon)
    norm_all = scalars[:, 2 * iters]
    last = (w_back / beta[:, None, None, None]) * norm_all[:, None, None, None]
    betas_all = jnp.concatenate([scalars[:, iters : 2 * iters - 1], beta[:, None]], axis=1)
    return scalars[:, :iters], betas_all, last


def solution(mesh):
    in_specs = (P(None, "trait", "tile", None), P("tile", None), P("tile", None), P())
    out_specs = (P(), P(), P(None, "trait", "tile", None))
    return jax.shard_map(shards, mesh=mesh, in_specs=in_specs, out_specs=out_specs, check_vma=False)
```

```python
import jax
import jax.numpy as jnp
from jax import lax
from jax.sharding import PartitionSpec as P


along_cols = 0.25
along_rows = 0.15
cross_term = 0.1
epsilon = 1e-06

HALO = 2


def nine_valid(x, kappa_rows):
    padded = jnp.pad(x, [(0, 0)] * (x.ndim - 1) + [(1, 1)])
    center = padded[..., 1:-1, 1:-1]
    sideways = padded[..., 1:-1, :-2] + padded[..., 1:-1, 2:]
    vertical = padded[..., :-2, 1:-1] + padded[..., 2:, 1:-1]
    diag_main = padded[..., 2:, 2:] + padded[..., :-2, :-2]
    diag_anti = padded[..., 2:, :-2] + padded[..., :-2, 2:]
    return (
        (kappa_rows + 2.0 * along_cols + 2.0 * along_rows) * center
        - along_cols * sideways
        - along_rows * vertical
        - 0.5 * cross_term * (diag_main - diag_anti)
    )


def gather_rows(v, axis):
    n = lax.axis_size(axis)
    return lax.all_to_all(jnp.concatenate([v] * n, axis=0), axis, 0, 0, tiled=True)


def tile_sum(v):
    n = lax.axis_size("tile")
    g = gather_rows(v, "tile").reshape((n,) + v.shape)
    return jnp.sum(g, axis=0)


def butterfly_sum(v, axis, work=()):
    n = lax.axis_size(axis)
    carry = None
    if n & (n - 1):
        for stage in work:
            carry = stage(carry)
        return lax.psum(v, axis), carry
    s = 1
    r = 0
    while s < n:
        got = lax.ppermute(v, axis, [(i, i ^ s) for i in range(n)])
        if r < len(work):
            carry = work[r](carry)
            v, carry = lax.optimization_barrier((v + got, carry))
        else:
            v = v + got
        s *= 2
        r += 1
    for stage in work[r:]:
        carry = stage(carry)
    return v, carry


def halo_rows(block, width):
    n = lax.axis_size("tile")
    dim = block.ndim - 2
    rows = block.shape[dim]
    assert rows >= width
    forward = [(i, i + 1) for i in range(n - 1)]
    backward = [(i + 1, i) for i in range(n - 1)]
    low = lax.ppermute(lax.slice_in_dim(block, rows - width, rows, axis=dim), "tile", forward)
    high = lax.ppermute(lax.slice_in_dim(block, 0, width, axis=dim), "tile", backward)
    return jnp.concatenate([low, block, high], axis=dim)


def shards(probe_signs, land_mask, kappa_sq, trait_covariance):
    rows = land_mask.shape[0]
    h = HALO
    signed = (land_mask[None, None] * (2 * probe_signs - 1)).astype(jnp.bfloat16)
    exchanged = lax.all_to_all(signed, "trait", split_axis=0, concat_axis=1, tiled=True)
    field_ext = halo_rows(exchanged, h).astype(jnp.float32)
    kappa_ext = halo_rows(kappa_sq, h)
    land_ext = field_ext[0, 0] * field_ext[0, 0]
    variances = jnp.diagonal(trait_covariance)
    z = field_ext * variances[None, :, None, None]

    def mix(x):
        return jnp.einsum("ts,psrc->ptrc", trait_covariance, x, precision=lax.Precision.HIGHEST)

    def stencil(x, off):
        r = x.shape[2]
        return land_ext[off + 1 : off + r - 1] * nine_valid(x, kappa_ext[off + 1 : off + r - 1])

    def apply_a(x, off):
        return mix(stencil(stencil(x, off), off + 1))

    def own(x):
        return x[:, :, h : h + rows]

    def reduce_tile(pairs, work=()):
        prods = jnp.stack([a * b for a, b in pairs], axis=-1)
        return butterfly_sum(jnp.sum(prods, axis=(1, 2, 3)), "tile", work)

    def a_stages(x):
        return (
            lambda _: halo_rows(x, h),
            lambda ext: stencil(ext, 0),
            lambda first: mix(stencil(first, 1)),
        )

    az = apply_a(z, 0)
    z = own(z)
    sums, aaz = reduce_tile([(z, z), (az, z)], a_stages(az))
    norm = jnp.sqrt(sums[:, 0] + epsilon)
    alpha = sums[:, 1] / (norm * norm)
    q = z / norm[:, None, None, None]
    aq = az / norm[:, None, None, None]
    w = aq - alpha[:, None, None, None] * q
    aw = aaz / norm[:, None, None, None] - alpha[:, None, None, None] * aq
    alphas = [alpha]
    betas = []
    iters = 3
    for step in range(1, iters):
        last_step = step == iters - 1
        sums, aaw = reduce_tile([(w, w), (aw, w), (q, w)], () if last_step else a_stages(aw))
        beta = jnp.sqrt(sums[:, 0] + epsilon)
        alpha = sums[:, 1] / (beta * beta) - sums[:, 2]
        q_next = w / beta[:, None, None, None]
        w_next = aw / beta[:, None, None, None] - beta[:, None, None, None] * q - alpha[:, None, None, None] * q_next
        if not last_step:
            aw_next = (
                aaw / beta[:, None, None, None]
                - beta[:, None, None, None] * aq
                - alpha[:, None, None, None] * aw / beta[:, None, None, None]
            )
            aq = aw / beta[:, None, None, None]
            aw = aw_next
        q = q_next
        w = w_next
        betas.append(beta)
        alphas.append(alpha)
    w_own = w
    w_back = lax.all_to_all(w_own, "trait", split_axis=1, concat_axis=0, tiled=True)
    partial = jnp.sum(w_own * w_own, axis=(1, 2, 3))[:, None]
    first = (lax.axis_index("tile") == 0).astype(jnp.float32)
    known = jnp.concatenate([jnp.stack(alphas, axis=1), jnp.stack(betas, axis=1)], axis=1)
    mine = jnp.concatenate([known * first, partial, norm[:, None] * first], axis=1)
    probes_local = mine.shape[0]
    n_trait = lax.axis_size("trait")
    spread = lax.dynamic_update_slice(
        jnp.zeros((probes_local * n_trait, mine.shape[1]), jnp.float32),
        mine,
        (lax.axis_index("trait") * probes_local, 0),
    )
    scalars = butterfly_sum(butterfly_sum(spread, "tile")[0], "trait")[0]
    beta = jnp.sqrt(scalars[:, 2 * iters - 1] + epsilon)
    norm_all = scalars[:, 2 * iters]
    last = (w_back / beta[:, None, None, None]) * norm_all[:, None, None, None]
    betas_all = jnp.concatenate([scalars[:, iters : 2 * iters - 1], beta[:, None]], axis=1)
    return scalars[:, :iters], betas_all, last


def solution(mesh):
    in_specs = (P(None, "trait", "tile", None), P("tile", None), P("tile", None), P())
    out_specs = (P(), P(), P(None, "trait", "tile", None))
    return jax.shard_map(shards, mesh=mesh, in_specs=in_specs, out_specs=out_specs, check_vma=False)
```

```python
import jax
import jax.numpy as jnp
from jax import lax
from jax.sharding import PartitionSpec as P


along_cols = 0.25
along_rows = 0.15
cross_term = 0.1
epsilon = 1e-06

HALO = 6


def nine_valid(x, kappa_rows):
    padded = jnp.pad(x, [(0, 0)] * (x.ndim - 1) + [(1, 1)])
    center = padded[..., 1:-1, 1:-1]
    sideways = padded[..., 1:-1, :-2] + padded[..., 1:-1, 2:]
    vertical = padded[..., :-2, 1:-1] + padded[..., 2:, 1:-1]
    diag_main = padded[..., 2:, 2:] + padded[..., :-2, :-2]
    diag_anti = padded[..., 2:, :-2] + padded[..., :-2, 2:]
    return (
        (kappa_rows + 2.0 * along_cols + 2.0 * along_rows) * center
        - along_cols * sideways
        - along_rows * vertical
        - 0.5 * cross_term * (diag_main - diag_anti)
    )


def butterfly_sum(v, axis, work=()):
    n = lax.axis_size(axis)
    carry = None
    if n & (n - 1):
        for stage in work:
            carry = stage(carry)
        return lax.psum(v, axis), carry
    s = 1
    r = 0
    while s < n:
        got = lax.ppermute(v, axis, [(i, i ^ s) for i in range(n)])
        if r < len(work):
            carry = work[r](carry)
            v, carry = lax.optimization_barrier((v + got, carry))
        else:
            v = v + got
        s *= 2
        r += 1
    for stage in work[r:]:
        carry = stage(carry)
    return v, carry


def halo_rows(block, width):
    n = lax.axis_size("tile")
    dim = block.ndim - 2
    rows = block.shape[dim]
    assert rows >= width and n % 2 == 0
    top = lax.slice_in_dim(block, 0, width, axis=dim)
    bottom = lax.slice_in_dim(block, rows - width, rows, axis=dim)
    odd = lax.axis_index("tile") % 2 == 1
    across = [(i, i + 1) for i in range(1, n - 1, 2)] + [(i + 1, i) for i in range(1, n - 1, 2)]
    within = [(i, i + 1) for i in range(0, n - 1, 2)] + [(i + 1, i) for i in range(0, n - 1, 2)]
    send = jnp.where(odd, bottom, top)
    pieces = 2 if width % 2 == 0 else 1
    step = width // pieces
    got_across = jnp.concatenate(
        [
            lax.ppermute(lax.slice_in_dim(send, k * step, (k + 1) * step, axis=dim), "tile", across)
            for k in range(pieces)
        ],
        axis=dim,
    )
    got_within = lax.ppermute(jnp.where(odd, top, bottom), "tile", within)
    low = jnp.where(odd, got_within, got_across)
    high = jnp.where(odd, got_across, got_within)
    return jnp.concatenate([low, block, high], axis=dim)


def shards(probe_signs, land_mask, kappa_sq, trait_covariance):
    rows = land_mask.shape[0]
    h = HALO
    signed = (land_mask[None, None] * (2 * probe_signs - 1)).astype(jnp.bfloat16)
    exchanged = lax.all_to_all(signed, "trait", split_axis=0, concat_axis=1, tiled=True)
    field_ext = halo_rows(exchanged, h).astype(jnp.float32)
    kappa_ext = halo_rows(kappa_sq, h)
    land_ext = field_ext[0, 0] * field_ext[0, 0]
    variances = jnp.diagonal(trait_covariance)
    z = field_ext * variances[None, :, None, None]

    def mix(x):
        return jnp.einsum("ts,psrc->ptrc", trait_covariance, x, precision=lax.Precision.HIGHEST)

    def stencil(x, off):
        r = x.shape[2]
        return land_ext[off + 1 : off + r - 1] * nine_valid(x, kappa_ext[off + 1 : off + r - 1])

    def apply_a(x, off):
        return mix(stencil(stencil(x, off), off + 1))

    def a_stages(x, off):
        return (lambda _: stencil(x, off), lambda first: mix(stencil(first, off + 1)))

    def own(x, off):
        return x[:, :, h - off : h - off + rows]

    def crop(x, k):
        return x[:, :, k : x.shape[2] - k]

    def reduce_tile(pairs, off, work=()):
        prods = jnp.stack([own(a, off) * own(b, off) for a, b in pairs], axis=-1)
        return butterfly_sum(jnp.sum(prods, axis=(1, 2, 3)), "tile", work)

    az = apply_a(z, 0)
    z2 = crop(z, 2)
    sums, aaz = reduce_tile([(z2, z2), (az, z2)], 2, a_stages(az, 2))
    norm = jnp.sqrt(sums[:, 0] + epsilon)
    alpha = sums[:, 1] / (norm * norm)
    q = z2 / norm[:, None, None, None]
    aq = az / norm[:, None, None, None]
    w = aq - alpha[:, None, None, None] * q
    aw = aaz / norm[:, None, None, None] - alpha[:, None, None, None] * crop(aq, 2)
    aq = crop(aq, 2)
    q = crop(q, 2)
    w = crop(w, 2)
    off = 4
    alphas = [alpha]
    betas = []
    iters = 3
    for step in range(1, iters):
        last_step = step == iters - 1
        sums, aaw = reduce_tile([(w, w), (aw, w), (q, w)], off, () if last_step else a_stages(aw, off))
        beta = jnp.sqrt(sums[:, 0] + epsilon)
        alpha = sums[:, 1] / (beta * beta) - sums[:, 2]
        q_next = w / beta[:, None, None, None]
        w_next = aw / beta[:, None, None, None] - beta[:, None, None, None] * q - alpha[:, None, None, None] * q_next
        if not last_step:
            aw_next = (
                aaw / beta[:, None, None, None]
                - beta[:, None, None, None] * crop(aq, 2)
                - alpha[:, None, None, None] * crop(aw, 2) / beta[:, None, None, None]
            )
            aq = crop(aw, 2) / beta[:, None, None, None]
            q = crop(q_next, 2)
            w = crop(w_next, 2)
            aw = aw_next
            off += 2
        else:
            q = q_next
            w = w_next
        betas.append(beta)
        alphas.append(alpha)
    w_own = own(w, off)
    w_back = lax.all_to_all(w_own, "trait", split_axis=1, concat_axis=0, tiled=True)
    partial = jnp.sum(w_own * w_own, axis=(1, 2, 3))[:, None]
    first = (lax.axis_index("tile") == 0).astype(jnp.float32)
    known = jnp.concatenate([jnp.stack(alphas, axis=1), jnp.stack(betas, axis=1)], axis=1)
    mine = jnp.concatenate([known * first, partial, norm[:, None] * first], axis=1)
    probes_local = mine.shape[0]
    n_trait = lax.axis_size("trait")
    spread = lax.dynamic_update_slice(
        jnp.zeros((probes_local * n_trait, mine.shape[1]), jnp.float32),
        mine,
        (lax.axis_index("trait") * probes_local, 0),
    )
    scalars = butterfly_sum(butterfly_sum(spread, "tile")[0], "trait")[0]
    beta = jnp.sqrt(scalars[:, 2 * iters - 1] + epsilon)
    norm_all = scalars[:, 2 * iters]
    last = (w_back / beta[:, None, None, None]) * norm_all[:, None, None, None]
    betas_all = jnp.concatenate([scalars[:, iters : 2 * iters - 1], beta[:, None]], axis=1)
    return scalars[:, :iters], betas_all, last


def solution(mesh):
    in_specs = (P(None, "trait", "tile", None), P("tile", None), P("tile", None), P())
    out_specs = (P(), P(), P(None, "trait", "tile", None))

    return jax.shard_map(shards, mesh=mesh, in_specs=in_specs, out_specs=out_specs, check_vma=False)
```

```python
import jax
import jax.numpy as jnp
from jax import lax
from jax.sharding import PartitionSpec as P


along_cols = 0.25
along_rows = 0.15
cross_term = 0.1
epsilon = 1e-06

HALO = 6


def nine_valid(x, kappa_rows):
    padded = jnp.pad(x, [(0, 0)] * (x.ndim - 1) + [(1, 1)])
    center = padded[..., 1:-1, 1:-1]
    sideways = padded[..., 1:-1, :-2] + padded[..., 1:-1, 2:]
    vertical = padded[..., :-2, 1:-1] + padded[..., 2:, 1:-1]
    diag_main = padded[..., 2:, 2:] + padded[..., :-2, :-2]
    diag_anti = padded[..., 2:, :-2] + padded[..., :-2, 2:]
    return (
        (kappa_rows + 2.0 * along_cols + 2.0 * along_rows) * center
        - along_cols * sideways
        - along_rows * vertical
        - 0.5 * cross_term * (diag_main - diag_anti)
    )


def butterfly_sum(v, axis, work=()):
    n = lax.axis_size(axis)
    carry = None
    if n & (n - 1):
        for stage in work:
            carry = stage(carry)
        return lax.psum(v, axis), carry
    s = 1
    r = 0
    while s < n:
        got = lax.ppermute(v, axis, [(i, i ^ s) for i in range(n)])
        if r < len(work):
            carry = work[r](carry)
            v, carry = lax.optimization_barrier((v + got, carry))
        else:
            v = v + got
        s *= 2
        r += 1
    for stage in work[r:]:
        carry = stage(carry)
    return v, carry


def halo_rows(block, width):
    n = lax.axis_size("tile")
    dim = block.ndim - 2
    rows = block.shape[dim]
    assert rows >= width and n % 2 == 0
    top = lax.slice_in_dim(block, 0, width, axis=dim)
    bottom = lax.slice_in_dim(block, rows - width, rows, axis=dim)
    odd = lax.axis_index("tile") % 2 == 1
    across = [(i, i + 1) for i in range(1, n - 1, 2)] + [(i + 1, i) for i in range(1, n - 1, 2)]
    within = [(i, i + 1) for i in range(0, n - 1, 2)] + [(i + 1, i) for i in range(0, n - 1, 2)]
    got_across = lax.ppermute(jnp.where(odd, bottom, top), "tile", across)
    got_within = lax.ppermute(jnp.where(odd, top, bottom), "tile", within)
    low = jnp.where(odd, got_within, got_across)
    high = jnp.where(odd, got_across, got_within)
    return jnp.concatenate([low, block, high], axis=dim)


def shards(probe_signs, land_mask, kappa_sq, trait_covariance):
    rows = land_mask.shape[0]
    h = HALO
    signed = (land_mask[None, None] * (2 * probe_signs - 1)).astype(jnp.bfloat16)
    exchanged = lax.all_to_all(signed, "trait", split_axis=0, concat_axis=1, tiled=True)
    field_ext = halo_rows(exchanged, h).astype(jnp.float32)
    kappa_ext = halo_rows(kappa_sq, h)
    land_ext = field_ext[0, 0] * field_ext[0, 0]
    variances = jnp.diagonal(trait_covariance)
    z = field_ext * variances[None, :, None, None]

    def mix(x):
        return jnp.einsum("ts,psrc->ptrc", trait_covariance, x, precision=lax.Precision.HIGHEST)

    def stencil(x, off):
        r = x.shape[2]
        return land_ext[off + 1 : off + r - 1] * nine_valid(x, kappa_ext[off + 1 : off + r - 1])

    def apply_a(x, off):
        return mix(stencil(stencil(x, off), off + 1))

    def a_stages(x, off):
        return (lambda _: stencil(x, off), lambda first: mix(stencil(first, off + 1)))

    def own(x, off):
        return x[:, :, h - off : h - off + rows]

    def crop(x, k):
        return x[:, :, k : x.shape[2] - k]

    def reduce_tile(pairs, off, work=()):
        prods = jnp.stack([own(a, off) * own(b, off) for a, b in pairs], axis=-1)
        return butterfly_sum(jnp.sum(prods, axis=(1, 2, 3)), "tile", work)

    az_own = apply_a(z[:, :, h - 2 : h + rows + 2], h - 2)
    zo = z[:, :, h : h + rows]

    def az_rest(_):
        low = apply_a(z[:, :, : h + 2], 0)
        high = apply_a(z[:, :, h + rows - 2 :], h + rows - 2)
        return jnp.concatenate([low, az_own, high], axis=2)

    stages = (
        az_rest,
        lambda az: (az, stencil(az, 2)),
        lambda got: (got[0], mix(stencil(got[1], 3))),
    )
    sums, (az, aaz) = reduce_tile([(zo, zo), (az_own, zo)], h, stages)
    z2 = crop(z, 2)
    norm = jnp.sqrt(sums[:, 0] + epsilon)
    alpha = sums[:, 1] / (norm * norm)
    q = z2 / norm[:, None, None, None]
    aq = az / norm[:, None, None, None]
    w = aq - alpha[:, None, None, None] * q
    aw = aaz / norm[:, None, None, None] - alpha[:, None, None, None] * crop(aq, 2)
    aq = crop(aq, 2)
    q = crop(q, 2)
    w = crop(w, 2)
    off = 4
    alphas = [alpha]
    betas = []
    iters = 3
    for step in range(1, iters):
        last_step = step == iters - 1
        sums, aaw = reduce_tile([(w, w), (aw, w), (q, w)], off, () if last_step else a_stages(aw, off))
        beta = jnp.sqrt(sums[:, 0] + epsilon)
        alpha = sums[:, 1] / (beta * beta) - sums[:, 2]
        q_next = w / beta[:, None, None, None]
        w_next = aw / beta[:, None, None, None] - beta[:, None, None, None] * q - alpha[:, None, None, None] * q_next
        if not last_step:
            aw_next = (
                aaw / beta[:, None, None, None]
                - beta[:, None, None, None] * crop(aq, 2)
                - alpha[:, None, None, None] * crop(aw, 2) / beta[:, None, None, None]
            )
            aq = crop(aw, 2) / beta[:, None, None, None]
            q = crop(q_next, 2)
            w = crop(w_next, 2)
            aw = aw_next
            off += 2
        else:
            q = q_next
            w = w_next
        betas.append(beta)
        alphas.append(alpha)
    w_own = own(w, off)
    w_back = lax.all_to_all(w_own, "trait", split_axis=1, concat_axis=0, tiled=True)
    partial = jnp.sum(w_own * w_own, axis=(1, 2, 3))[:, None]
    first = (lax.axis_index("tile") == 0).astype(jnp.float32)
    known = jnp.concatenate([jnp.stack(alphas, axis=1), jnp.stack(betas, axis=1)], axis=1)
    mine = jnp.concatenate([known * first, partial, norm[:, None] * first], axis=1)
    probes_local = mine.shape[0]
    n_trait = lax.axis_size("trait")
    spread = lax.dynamic_update_slice(
        jnp.zeros((probes_local * n_trait, mine.shape[1]), jnp.float32),
        mine,
        (lax.axis_index("trait") * probes_local, 0),
    )
    scalars = butterfly_sum(butterfly_sum(spread, "tile")[0], "trait")[0]
    beta = jnp.sqrt(scalars[:, 2 * iters - 1] + epsilon)
    norm_all = scalars[:, 2 * iters]
    last = (w_back / beta[:, None, None, None]) * norm_all[:, None, None, None]
    betas_all = jnp.concatenate([scalars[:, iters : 2 * iters - 1], beta[:, None]], axis=1)
    return scalars[:, :iters], betas_all, last


def solution(mesh):
    in_specs = (P(None, "trait", "tile", None), P("tile", None), P("tile", None), P())
    out_specs = (P(), P(), P(None, "trait", "tile", None))

    return jax.shard_map(shards, mesh=mesh, in_specs=in_specs, out_specs=out_specs, check_vma=False)
```

```python
import jax
import jax.numpy as jnp
from jax import lax
from jax.sharding import PartitionSpec as P


along_cols = 0.25
along_rows = 0.15
cross_term = 0.1
epsilon = 1e-06

HALO = 6


def nine_valid(x, kappa_rows):
    padded = jnp.pad(x, [(0, 0)] * (x.ndim - 1) + [(1, 1)])
    center = padded[..., 1:-1, 1:-1]
    sideways = padded[..., 1:-1, :-2] + padded[..., 1:-1, 2:]
    vertical = padded[..., :-2, 1:-1] + padded[..., 2:, 1:-1]
    diag_main = padded[..., 2:, 2:] + padded[..., :-2, :-2]
    diag_anti = padded[..., 2:, :-2] + padded[..., :-2, 2:]
    return (
        (kappa_rows + 2.0 * along_cols + 2.0 * along_rows) * center
        - along_cols * sideways
        - along_rows * vertical
        - 0.5 * cross_term * (diag_main - diag_anti)
    )


def butterfly_sum(v, axis, work=()):
    n = lax.axis_size(axis)
    carry = None
    if n & (n - 1):
        for stage in work:
            carry = stage(carry)
        return lax.psum(v, axis), carry
    s = 1
    r = 0
    while s < n:
        got = lax.ppermute(v, axis, [(i, i ^ s) for i in range(n)])
        if r < len(work):
            carry = work[r](carry)
            v, carry = lax.optimization_barrier((v + got, carry))
        else:
            v = v + got
        s *= 2
        r += 1
    for stage in work[r:]:
        carry = stage(carry)
    return v, carry


def halo_rows(block, width):
    n = lax.axis_size("tile")
    dim = block.ndim - 2
    rows = block.shape[dim]
    assert rows >= width and n % 2 == 0
    top = lax.slice_in_dim(block, 0, width, axis=dim)
    bottom = lax.slice_in_dim(block, rows - width, rows, axis=dim)
    odd = lax.axis_index("tile") % 2 == 1
    across = [(i, i + 1) for i in range(1, n - 1, 2)] + [(i + 1, i) for i in range(1, n - 1, 2)]
    within = [(i, i + 1) for i in range(0, n - 1, 2)] + [(i + 1, i) for i in range(0, n - 1, 2)]
    got_across = lax.ppermute(jnp.where(odd, bottom, top), "tile", across)
    got_within = lax.ppermute(jnp.where(odd, top, bottom), "tile", within)
    low = jnp.where(odd, got_within, got_across)
    high = jnp.where(odd, got_across, got_within)
    return jnp.concatenate([low, block, high], axis=dim)


def shards(probe_signs, land_mask, kappa_sq, trait_covariance):
    rows = land_mask.shape[0]
    h = HALO
    signed = (land_mask[None, None] * (2 * probe_signs - 1)).astype(jnp.bfloat16)
    exchanged = lax.all_to_all(signed, "trait", split_axis=0, concat_axis=1, tiled=True)
    field_ext = halo_rows(exchanged, h).astype(jnp.float32)
    kappa_ext = halo_rows(kappa_sq, h)
    land_ext = field_ext[0, 0] * field_ext[0, 0]
    variances = jnp.diagonal(trait_covariance)
    z = field_ext * variances[None, :, None, None]

    def mix(x):
        return jnp.einsum("ts,psrc->ptrc", trait_covariance, x, precision=lax.Precision.HIGHEST)

    def stencil(x, off):
        r = x.shape[2]
        return land_ext[off + 1 : off + r - 1] * nine_valid(x, kappa_ext[off + 1 : off + r - 1])

    def apply_a(x, off):
        return mix(stencil(stencil(x, off), off + 1))

    def a_stages(x, off):
        return (lambda _: stencil(x, off), lambda first: mix(stencil(first, off + 1)))

    def own(x, off):
        return x[:, :, h - off : h - off + rows]

    def crop(x, k):
        return x[:, :, k : x.shape[2] - k]

    def reduce_tile(pairs, off, work=()):
        prods = jnp.stack([own(a, off) * own(b, off) for a, b in pairs], axis=-1)
        return butterfly_sum(jnp.sum(prods, axis=(1, 2, 3)), "tile", work)

    az = apply_a(z, 0)
    z2 = crop(z, 2)
    sums, aaz = reduce_tile([(z2, z2), (az, z2)], 2, a_stages(az, 2))
    norm = jnp.sqrt(sums[:, 0] + epsilon)
    alpha = sums[:, 1] / (norm * norm)
    q = z2 / norm[:, None, None, None]
    aq = az / norm[:, None, None, None]
    w = aq - alpha[:, None, None, None] * q
    aw = aaz / norm[:, None, None, None] - alpha[:, None, None, None] * crop(aq, 2)
    aq = crop(aq, 2)
    q = crop(q, 2)
    w = crop(w, 2)
    off = 4
    alphas = [alpha]
    betas = []
    iters = 3
    for step in range(1, iters):
        last_step = step == iters - 1
        sums, aaw = reduce_tile([(w, w), (aw, w), (q, w)], off, () if last_step else a_stages(aw, off))
        beta = jnp.sqrt(sums[:, 0] + epsilon)
        alpha = sums[:, 1] / (beta * beta) - sums[:, 2]
        q_next = w / beta[:, None, None, None]
        w_next = aw / beta[:, None, None, None] - beta[:, None, None, None] * q - alpha[:, None, None, None] * q_next
        if not last_step:
            aw_next = (
                aaw / beta[:, None, None, None]
                - beta[:, None, None, None] * crop(aq, 2)
                - alpha[:, None, None, None] * crop(aw, 2) / beta[:, None, None, None]
            )
            aq = crop(aw, 2) / beta[:, None, None, None]
            q = crop(q_next, 2)
            w = crop(w_next, 2)
            aw = aw_next
            off += 2
        else:
            q = q_next
            w = w_next
        betas.append(beta)
        alphas.append(alpha)
    w_own = own(w, off)
    w_back = lax.all_to_all(w_own, "trait", split_axis=1, concat_axis=0, tiled=True)
    partial = jnp.sum(w_own * w_own, axis=(1, 2, 3))[:, None]
    first = (lax.axis_index("tile") == 0).astype(jnp.float32)
    known = jnp.concatenate([jnp.stack(alphas, axis=1), jnp.stack(betas, axis=1)], axis=1)
    mine = jnp.concatenate([known * first, partial, norm[:, None] * first], axis=1)
    probes_local = mine.shape[0]
    n_trait = lax.axis_size("trait")
    spread = lax.dynamic_update_slice(
        jnp.zeros((probes_local * n_trait, mine.shape[1]), jnp.float32),
        mine,
        (lax.axis_index("trait") * probes_local, 0),
    )
    scalars = butterfly_sum(spread, "tile")[0]
    scalars = butterfly_sum(scalars, "trait")[0]
    beta = jnp.sqrt(scalars[:, 2 * iters - 1] + epsilon)
    norm_all = scalars[:, 2 * iters]
    last = (w_back / beta[:, None, None, None]) * norm_all[:, None, None, None]
    betas_all = jnp.concatenate([scalars[:, iters : 2 * iters - 1], beta[:, None]], axis=1)
    return scalars[:, :iters], betas_all, last


def solution(mesh):
    in_specs = (P(None, "trait", "tile", None), P("tile", None), P("tile", None), P())
    out_specs = (P(), P(), P(None, "trait", "tile", None))

    return jax.shard_map(shards, mesh=mesh, in_specs=in_specs, out_specs=out_specs, check_vma=False)
```

```python
import jax
import jax.numpy as jnp
from jax import lax
from jax.sharding import PartitionSpec as P


along_cols = 0.25
along_rows = 0.15
cross_term = 0.1
epsilon = 1e-06

HALO = 6


def nine_valid(x, kappa_rows):
    padded = jnp.pad(x, [(0, 0)] * (x.ndim - 1) + [(1, 1)])
    center = padded[..., 1:-1, 1:-1]
    sideways = padded[..., 1:-1, :-2] + padded[..., 1:-1, 2:]
    vertical = padded[..., :-2, 1:-1] + padded[..., 2:, 1:-1]
    diag_main = padded[..., 2:, 2:] + padded[..., :-2, :-2]
    diag_anti = padded[..., 2:, :-2] + padded[..., :-2, 2:]
    return (
        (kappa_rows + 2.0 * along_cols + 2.0 * along_rows) * center
        - along_cols * sideways
        - along_rows * vertical
        - 0.5 * cross_term * (diag_main - diag_anti)
    )


def butterfly_sum(v, axis, work=()):
    n = lax.axis_size(axis)
    carry = None
    if n & (n - 1):
        for stage in work:
            carry = stage(carry)
        return lax.psum(v, axis), carry
    s = 1
    r = 0
    while s < n:
        got = lax.ppermute(v, axis, [(i, i ^ s) for i in range(n)])
        if r < len(work):
            carry = work[r](carry)
            v, carry = lax.optimization_barrier((v + got, carry))
        else:
            v = v + got
        s *= 2
        r += 1
    for stage in work[r:]:
        carry = stage(carry)
    return v, carry


def halo_rows(block, width):
    n = lax.axis_size("tile")
    dim = block.ndim - 2
    rows = block.shape[dim]
    assert rows >= width and n % 2 == 0
    top = lax.slice_in_dim(block, 0, width, axis=dim)
    bottom = lax.slice_in_dim(block, rows - width, rows, axis=dim)
    odd = lax.axis_index("tile") % 2 == 1
    across = [(i, i + 1) for i in range(1, n - 1, 2)] + [(i + 1, i) for i in range(1, n - 1, 2)]
    within = [(i, i + 1) for i in range(0, n - 1, 2)] + [(i + 1, i) for i in range(0, n - 1, 2)]
    got_across = lax.ppermute(jnp.where(odd, bottom, top), "tile", across)
    got_within = lax.ppermute(jnp.where(odd, top, bottom), "tile", within)
    low = jnp.where(odd, got_within, got_across)
    high = jnp.where(odd, got_across, got_within)
    return jnp.concatenate([low, block, high], axis=dim)


def shards(probe_signs, land_mask, kappa_sq, trait_covariance):
    rows = land_mask.shape[0]
    h = HALO
    signed = (land_mask[None, None] * (2 * probe_signs - 1)).astype(jnp.bfloat16)
    exchanged = lax.all_to_all(signed, "trait", split_axis=0, concat_axis=1, tiled=True)
    field_ext = halo_rows(exchanged, h).astype(jnp.float32)
    kappa_ext = halo_rows(kappa_sq, h)
    land_ext = field_ext[0, 0] * field_ext[0, 0]
    variances = jnp.diagonal(trait_covariance)
    z = field_ext * variances[None, :, None, None]

    def mix(x):
        return jnp.einsum("ts,psrc->ptrc", trait_covariance, x, precision=lax.Precision.HIGHEST)

    def stencil(x, off):
        r = x.shape[2]
        return land_ext[off + 1 : off + r - 1] * nine_valid(x, kappa_ext[off + 1 : off + r - 1])

    def apply_a(x, off):
        return mix(stencil(stencil(x, off), off + 1))

    def a_stages(x, off):
        return (lambda _: stencil(x, off), lambda first: mix(stencil(first, off + 1)))

    def own(x, off):
        return x[:, :, h - off : h - off + rows]

    def lanes(v):
        return lax.optimization_barrier(jnp.broadcast_to(v[:, :, None], v.shape + (128,)))

    def crop(x, k):
        return x[:, :, k : x.shape[2] - k]

    def reduce_tile(pairs, off, work=()):
        prods = jnp.stack([own(a, off) * own(b, off) for a, b in pairs], axis=-1)
        return butterfly_sum(jnp.sum(prods, axis=(1, 2, 3)), "tile", work)

    az = apply_a(z, 0)
    z2 = crop(z, 2)
    sums, aaz = reduce_tile([(z2, z2), (az, z2)], 2, a_stages(az, 2))
    sv = lanes(sums)
    norm_v = jnp.sqrt(sv[:, 0] + epsilon)
    alpha_v = sv[:, 1] / (norm_v * norm_v)
    norm = norm_v[:, 0]
    alpha = alpha_v[:, 0]
    q = z2 / norm[:, None, None, None]
    aq = az / norm[:, None, None, None]
    w = aq - alpha[:, None, None, None] * q
    aw = aaz / norm[:, None, None, None] - alpha[:, None, None, None] * crop(aq, 2)
    aq = crop(aq, 2)
    q = crop(q, 2)
    w = crop(w, 2)
    off = 4
    alphas = [alpha]
    betas = []
    iters = 3
    for step in range(1, iters):
        last_step = step == iters - 1
        sums, aaw = reduce_tile([(w, w), (aw, w), (q, w)], off, () if last_step else a_stages(aw, off))
        sv = lanes(sums)
        beta_v = jnp.sqrt(sv[:, 0] + epsilon)
        alpha_v = sv[:, 1] / (beta_v * beta_v) - sv[:, 2]
        beta = beta_v[:, 0]
        alpha = alpha_v[:, 0]
        q_next = w / beta[:, None, None, None]
        w_next = aw / beta[:, None, None, None] - beta[:, None, None, None] * q - alpha[:, None, None, None] * q_next
        if not last_step:
            aw_next = (
                aaw / beta[:, None, None, None]
                - beta[:, None, None, None] * crop(aq, 2)
                - alpha[:, None, None, None] * crop(aw, 2) / beta[:, None, None, None]
            )
            aq = crop(aw, 2) / beta[:, None, None, None]
            q = crop(q_next, 2)
            w = crop(w_next, 2)
            aw = aw_next
            off += 2
        else:
            q = q_next
            w = w_next
        betas.append(beta)
        alphas.append(alpha)
    w_own = own(w, off)
    w_back = lax.all_to_all(w_own, "trait", split_axis=1, concat_axis=0, tiled=True)
    partial = jnp.sum(w_own * w_own, axis=(1, 2, 3))[:, None]
    first = (lax.axis_index("tile") == 0).astype(jnp.float32)
    known = jnp.concatenate([jnp.stack(alphas, axis=1), jnp.stack(betas, axis=1)], axis=1)
    mine = jnp.concatenate([known * first, partial, norm[:, None] * first], axis=1)
    probes_local = mine.shape[0]
    n_trait = lax.axis_size("trait")
    spread = lax.dynamic_update_slice(
        jnp.zeros((probes_local * n_trait, mine.shape[1]), jnp.float32),
        mine,
        (lax.axis_index("trait") * probes_local, 0),
    )
    scalars = butterfly_sum(butterfly_sum(spread, "tile")[0], "trait")[0]
    beta = jnp.sqrt(scalars[:, 2 * iters - 1] + epsilon)
    norm_all = scalars[:, 2 * iters]
    last = (w_back / beta[:, None, None, None]) * norm_all[:, None, None, None]
    betas_all = jnp.concatenate([scalars[:, iters : 2 * iters - 1], beta[:, None]], axis=1)
    return scalars[:, :iters], betas_all, last


def solution(mesh):
    in_specs = (P(None, "trait", "tile", None), P("tile", None), P("tile", None), P())
    out_specs = (P(), P(), P(None, "trait", "tile", None))

    return jax.shard_map(shards, mesh=mesh, in_specs=in_specs, out_specs=out_specs, check_vma=False)
```

```python
import jax
import jax.numpy as jnp
from jax import lax
from jax.sharding import PartitionSpec as P


along_cols = 0.25
along_rows = 0.15
cross_term = 0.1
epsilon = 1e-06

HALO = 6


def nine_valid(x, kappa_rows):
    padded = jnp.pad(x, [(0, 0)] * (x.ndim - 1) + [(1, 1)])
    center = padded[..., 1:-1, 1:-1]
    sideways = padded[..., 1:-1, :-2] + padded[..., 1:-1, 2:]
    vertical = padded[..., :-2, 1:-1] + padded[..., 2:, 1:-1]
    diag_main = padded[..., 2:, 2:] + padded[..., :-2, :-2]
    diag_anti = padded[..., 2:, :-2] + padded[..., :-2, 2:]
    return (
        (kappa_rows + 2.0 * along_cols + 2.0 * along_rows) * center
        - along_cols * sideways
        - along_rows * vertical
        - 0.5 * cross_term * (diag_main - diag_anti)
    )


def butterfly_sum(v, axis, work=()):
    n = lax.axis_size(axis)
    carry = None
    if n & (n - 1):
        for stage in work:
            carry = stage(carry)
        return lax.psum(v, axis), carry
    s = 1
    r = 0
    while s < n:
        got = lax.ppermute(v, axis, [(i, i ^ s) for i in range(n)])
        if r < len(work):
            carry = work[r](carry)
            v, carry = lax.optimization_barrier((v + got, carry))
        else:
            v = v + got
        s *= 2
        r += 1
    for stage in work[r:]:
        carry = stage(carry)
    return v, carry


def halo_rows(block, width):
    n = lax.axis_size("tile")
    dim = block.ndim - 2
    rows = block.shape[dim]
    assert rows >= width and n % 2 == 0
    top = lax.slice_in_dim(block, 0, width, axis=dim)
    bottom = lax.slice_in_dim(block, rows - width, rows, axis=dim)
    odd = lax.axis_index("tile") % 2 == 1
    across = [(i, i + 1) for i in range(1, n - 1, 2)] + [(i + 1, i) for i in range(1, n - 1, 2)]
    within = [(i, i + 1) for i in range(0, n - 1, 2)] + [(i + 1, i) for i in range(0, n - 1, 2)]
    got_across = lax.ppermute(jnp.where(odd, bottom, top), "tile", across)
    got_within = lax.ppermute(jnp.where(odd, top, bottom), "tile", within)
    low = jnp.where(odd, got_within, got_across)
    high = jnp.where(odd, got_across, got_within)
    return jnp.concatenate([low, block, high], axis=dim)


def shards(probe_signs, land_mask, kappa_sq, trait_covariance):
    rows = land_mask.shape[0]
    h = HALO
    signed = (land_mask[None, None] * (2 * probe_signs - 1)).astype(jnp.bfloat16)
    exchanged = lax.all_to_all(signed, "trait", split_axis=0, concat_axis=1, tiled=True)
    field_ext = halo_rows(exchanged, h).astype(jnp.float32)
    kappa_ext = halo_rows(kappa_sq, h)
    land_ext = field_ext[0, 0] * field_ext[0, 0]
    variances = jnp.diagonal(trait_covariance)
    z = field_ext * variances[None, :, None, None]

    def mix(x):
        return jnp.einsum("ts,psrc->ptrc", trait_covariance, x, precision=lax.Precision.HIGHEST)

    def stencil(x, off):
        r = x.shape[2]
        return land_ext[off + 1 : off + r - 1] * nine_valid(x, kappa_ext[off + 1 : off + r - 1])

    def apply_a(x, off):
        return mix(stencil(stencil(x, off), off + 1))

    def a_stages(x, off):
        return (lambda _: stencil(x, off), lambda first: mix(stencil(first, off + 1)))

    def own(x, off):
        return x[:, :, h - off : h - off + rows]

    def lanes(v):
        return lax.optimization_barrier(jnp.broadcast_to(v[:, :, None], v.shape + (128,)))

    def crop(x, k):
        return x[:, :, k : x.shape[2] - k]

    def reduce_tile(pairs, off, work=()):
        prods = jnp.stack([own(a, off) * own(b, off) for a, b in pairs], axis=-1)
        return butterfly_sum(jnp.sum(prods, axis=(1, 2, 3)), "tile", work)

    az = apply_a(z, 0)
    z2 = crop(z, 2)
    sums, aaz = reduce_tile([(z2, z2), (az, z2)], 2, a_stages(az, 2))
    sv = lanes(sums)
    norm_v = jnp.sqrt(sv[:, 0] + epsilon)
    alpha_v = sv[:, 1] / (norm_v * norm_v)
    norm = norm_v[:, 0]
    alpha = alpha_v[:, 0]
    q = z2 / norm[:, None, None, None]
    aq = az / norm[:, None, None, None]
    w = aq - alpha[:, None, None, None] * q
    aw = aaz / norm[:, None, None, None] - alpha[:, None, None, None] * crop(aq, 2)
    aq = crop(aq, 2)
    q = crop(q, 2)
    w = crop(w, 2)
    off = 4
    alphas = [alpha]
    betas = []
    iters = 3
    for step in range(1, iters):
        last_step = step == iters - 1
        sums, aaw = reduce_tile([(w, w), (aw, w), (q, w)], off, () if last_step else a_stages(aw, off))
        sv = lanes(sums)
        beta_v = jnp.sqrt(sv[:, 0] + epsilon)
        alpha_v = sv[:, 1] / (beta_v * beta_v) - sv[:, 2]
        beta = beta_v[:, 0]
        alpha = alpha_v[:, 0]
        q_next = w / beta[:, None, None, None]
        w_next = aw / beta[:, None, None, None] - beta[:, None, None, None] * q - alpha[:, None, None, None] * q_next
        if not last_step:
            aw_next = (
                aaw / beta[:, None, None, None]
                - beta[:, None, None, None] * crop(aq, 2)
                - alpha[:, None, None, None] * crop(aw, 2) / beta[:, None, None, None]
            )
            aq = crop(aw, 2) / beta[:, None, None, None]
            q = crop(q_next, 2)
            w = crop(w_next, 2)
            aw = aw_next
            off += 2
        else:
            q = q_next
            w = w_next
        betas.append(beta)
        alphas.append(alpha)
    w_own = own(w, off)
    w_back = lax.all_to_all(w_own, "trait", split_axis=1, concat_axis=0, tiled=True)
    partial = jnp.sum(w_own * w_own, axis=(1, 2, 3))[:, None]
    first = (lax.axis_index("tile") == 0).astype(jnp.float32)
    known = jnp.concatenate([jnp.stack(alphas, axis=1), jnp.stack(betas, axis=1)], axis=1)
    mine = jnp.concatenate([known * first, partial, norm[:, None] * first], axis=1)
    probes_local = mine.shape[0]
    n_trait = lax.axis_size("trait")
    spread = lax.dynamic_update_slice(
        jnp.zeros((probes_local * n_trait, mine.shape[1]), jnp.float32),
        mine,
        (lax.axis_index("trait") * probes_local, 0),
    )
    scalars = butterfly_sum(spread, "tile")[0]
    n_t = lax.axis_size("trait")
    shifted = [lax.ppermute(scalars, "trait", [(i, (i + d) % n_t) for i in range(n_t)]) for d in range(1, n_t)]
    for got in shifted:
        scalars = scalars + got
    beta = jnp.sqrt(scalars[:, 2 * iters - 1] + epsilon)
    norm_all = scalars[:, 2 * iters]
    last = (w_back / beta[:, None, None, None]) * norm_all[:, None, None, None]
    betas_all = jnp.concatenate([scalars[:, iters : 2 * iters - 1], beta[:, None]], axis=1)
    return scalars[:, :iters], betas_all, last


def solution(mesh):
    in_specs = (P(None, "trait", "tile", None), P("tile", None), P("tile", None), P())
    out_specs = (P(), P(), P(None, "trait", "tile", None))

    return jax.shard_map(shards, mesh=mesh, in_specs=in_specs, out_specs=out_specs, check_vma=False)
```

```python
import jax
import jax.numpy as jnp
from jax import lax
from jax.sharding import PartitionSpec as P


along_cols = 0.25
along_rows = 0.15
cross_term = 0.1
epsilon = 1e-06

HALO = 6


def nine_valid(x, kappa_rows):
    padded = jnp.pad(x, [(0, 0)] * (x.ndim - 1) + [(1, 1)])
    center = padded[..., 1:-1, 1:-1]
    sideways = padded[..., 1:-1, :-2] + padded[..., 1:-1, 2:]
    vertical = padded[..., :-2, 1:-1] + padded[..., 2:, 1:-1]
    diag_main = padded[..., 2:, 2:] + padded[..., :-2, :-2]
    diag_anti = padded[..., 2:, :-2] + padded[..., :-2, 2:]
    return (
        (kappa_rows + 2.0 * along_cols + 2.0 * along_rows) * center
        - along_cols * sideways
        - along_rows * vertical
        - 0.5 * cross_term * (diag_main - diag_anti)
    )


def butterfly_sum(v, axis, work=()):
    n = lax.axis_size(axis)
    carry = None
    if n & (n - 1):
        for stage in work:
            carry = stage(carry)
        return lax.psum(v, axis), carry
    s = 1
    r = 0
    while s < n:
        got = lax.ppermute(v, axis, [(i, i ^ s) for i in range(n)])
        if r < len(work):
            carry = work[r](carry)
            v, carry = lax.optimization_barrier((v + got, carry))
        else:
            v = v + got
        s *= 2
        r += 1
    for stage in work[r:]:
        carry = stage(carry)
    return v, carry


def halo_rows(block, width):
    n = lax.axis_size("tile")
    dim = block.ndim - 2
    rows = block.shape[dim]
    assert rows >= width and n % 2 == 0
    top = lax.slice_in_dim(block, 0, width, axis=dim)
    bottom = lax.slice_in_dim(block, rows - width, rows, axis=dim)
    odd = lax.axis_index("tile") % 2 == 1
    across = [(i, i + 1) for i in range(1, n - 1, 2)] + [(i + 1, i) for i in range(1, n - 1, 2)]
    within = [(i, i + 1) for i in range(0, n - 1, 2)] + [(i + 1, i) for i in range(0, n - 1, 2)]
    got_across = lax.ppermute(jnp.where(odd, bottom, top), "tile", across)
    got_within = lax.ppermute(jnp.where(odd, top, bottom), "tile", within)
    low = jnp.where(odd, got_within, got_across)
    high = jnp.where(odd, got_across, got_within)
    return jnp.concatenate([low, block, high], axis=dim)


def shards(probe_signs, land_mask, kappa_sq, trait_covariance):
    rows = land_mask.shape[0]
    h = HALO
    signed = (land_mask[None, None] * (2 * probe_signs - 1)).astype(jnp.bfloat16)
    exchanged = lax.all_to_all(signed, "trait", split_axis=0, concat_axis=1, tiled=True)
    field_ext = halo_rows(exchanged, h).astype(jnp.float32)
    kappa_ext = halo_rows(kappa_sq, h)
    land_ext = field_ext[0, 0] * field_ext[0, 0]
    variances = jnp.diagonal(trait_covariance)
    z = field_ext * variances[None, :, None, None]

    def mix(x):
        return jnp.einsum("ts,psrc->ptrc", trait_covariance, x, precision=lax.Precision.HIGHEST)

    def stencil(x, off):
        r = x.shape[2]
        return land_ext[off + 1 : off + r - 1] * nine_valid(x, kappa_ext[off + 1 : off + r - 1])

    def apply_a(x, off):
        return mix(stencil(stencil(x, off), off + 1))

    def a_stages(x, off, split_mix=False):
        if split_mix:
            return (lambda _: stencil(x, off), lambda first: stencil(first, off + 1), mix)
        return (lambda _: stencil(x, off), lambda first: mix(stencil(first, off + 1)))

    def own(x, off):
        return x[:, :, h - off : h - off + rows]

    def lanes(v):
        return lax.optimization_barrier(jnp.broadcast_to(v[:, :, None], v.shape + (128,)))

    def crop(x, k):
        return x[:, :, k : x.shape[2] - k]

    def reduce_tile(pairs, off, work=()):
        prods = jnp.stack([own(a, off) * own(b, off) for a, b in pairs], axis=-1)
        return butterfly_sum(jnp.sum(prods, axis=(1, 2, 3)), "tile", work)

    az = apply_a(z, 0)
    z2 = crop(z, 2)
    sums, aaz = reduce_tile([(z2, z2), (az, z2)], 2, a_stages(az, 2, split_mix=True))
    sv = lanes(sums)
    norm_v = jnp.sqrt(sv[:, 0] + epsilon)
    alpha_v = sv[:, 1] / (norm_v * norm_v)
    norm = norm_v[:, 0]
    alpha = alpha_v[:, 0]
    q = z2 / norm[:, None, None, None]
    aq = az / norm[:, None, None, None]
    w = aq - alpha[:, None, None, None] * q
    aw = aaz / norm[:, None, None, None] - alpha[:, None, None, None] * crop(aq, 2)
    aq = crop(aq, 2)
    q = crop(q, 2)
    w = crop(w, 2)
    off = 4
    alphas = [alpha]
    betas = []
    iters = 3
    for step in range(1, iters):
        last_step = step == iters - 1
        sums, aaw = reduce_tile([(w, w), (aw, w), (q, w)], off, () if last_step else a_stages(aw, off, split_mix=True))
        sv = lanes(sums)
        beta_v = jnp.sqrt(sv[:, 0] + epsilon)
        alpha_v = sv[:, 1] / (beta_v * beta_v) - sv[:, 2]
        beta = beta_v[:, 0]
        alpha = alpha_v[:, 0]
        q_next = w / beta[:, None, None, None]
        w_next = aw / beta[:, None, None, None] - beta[:, None, None, None] * q - alpha[:, None, None, None] * q_next
        if not last_step:
            aw_next = (
                aaw / beta[:, None, None, None]
                - beta[:, None, None, None] * crop(aq, 2)
                - alpha[:, None, None, None] * crop(aw, 2) / beta[:, None, None, None]
            )
            aq = crop(aw, 2) / beta[:, None, None, None]
            q = crop(q_next, 2)
            w = crop(w_next, 2)
            aw = aw_next
            off += 2
        else:
            q = q_next
            w = w_next
        betas.append(beta)
        alphas.append(alpha)
    w_own = own(w, off)
    w_back = lax.all_to_all(w_own, "trait", split_axis=1, concat_axis=0, tiled=True)
    partial = jnp.sum(w_own * w_own, axis=(1, 2, 3))[:, None]
    first = (lax.axis_index("tile") == 0).astype(jnp.float32)
    known = jnp.concatenate([jnp.stack(alphas, axis=1), jnp.stack(betas, axis=1)], axis=1)
    mine = jnp.concatenate([known * first, partial, norm[:, None] * first], axis=1)
    probes_local = mine.shape[0]
    n_trait = lax.axis_size("trait")
    spread = lax.dynamic_update_slice(
        jnp.zeros((probes_local * n_trait, mine.shape[1]), jnp.float32),
        mine,
        (lax.axis_index("trait") * probes_local, 0),
    )
    scalars = butterfly_sum(butterfly_sum(spread, "tile")[0], "trait")[0]
    beta = jnp.sqrt(scalars[:, 2 * iters - 1] + epsilon)
    norm_all = scalars[:, 2 * iters]
    last = (w_back / beta[:, None, None, None]) * norm_all[:, None, None, None]
    betas_all = jnp.concatenate([scalars[:, iters : 2 * iters - 1], beta[:, None]], axis=1)
    return scalars[:, :iters], betas_all, last


def solution(mesh):
    in_specs = (P(None, "trait", "tile", None), P("tile", None), P("tile", None), P())
    out_specs = (P(), P(), P(None, "trait", "tile", None))

    return jax.shard_map(shards, mesh=mesh, in_specs=in_specs, out_specs=out_specs, check_vma=False)
```

```python
import jax
import jax.numpy as jnp
from jax import lax
from jax.sharding import PartitionSpec as P


along_cols = 0.25
along_rows = 0.15
cross_term = 0.1
epsilon = 1e-06

HALO = 6


def nine_valid(x, kappa_rows):
    padded = jnp.pad(x, [(0, 0)] * (x.ndim - 1) + [(1, 1)])
    center = padded[..., 1:-1, 1:-1]
    sideways = padded[..., 1:-1, :-2] + padded[..., 1:-1, 2:]
    vertical = padded[..., :-2, 1:-1] + padded[..., 2:, 1:-1]
    diag_main = padded[..., 2:, 2:] + padded[..., :-2, :-2]
    diag_anti = padded[..., 2:, :-2] + padded[..., :-2, 2:]
    return (
        (kappa_rows + 2.0 * along_cols + 2.0 * along_rows) * center
        - along_cols * sideways
        - along_rows * vertical
        - 0.5 * cross_term * (diag_main - diag_anti)
    )


def butterfly_sum(v, axis, work=()):
    n = lax.axis_size(axis)
    carry = None
    if n & (n - 1):
        for stage in work:
            carry = stage(carry)
        return lax.psum(v, axis), carry
    s = 1
    r = 0
    while s < n:
        got = lax.ppermute(v, axis, [(i, i ^ s) for i in range(n)])
        if r < len(work):
            carry = work[r](carry)
            v, carry = lax.optimization_barrier((v + got, carry))
        else:
            v = v + got
        s *= 2
        r += 1
    for stage in work[r:]:
        carry = stage(carry)
    return v, carry


def halo_rows(block, width):
    n = lax.axis_size("tile")
    dim = block.ndim - 2
    rows = block.shape[dim]
    assert rows >= width and n % 2 == 0
    top = lax.slice_in_dim(block, 0, width, axis=dim)
    bottom = lax.slice_in_dim(block, rows - width, rows, axis=dim)
    odd = lax.axis_index("tile") % 2 == 1
    across = [(i, i + 1) for i in range(1, n - 1, 2)] + [(i + 1, i) for i in range(1, n - 1, 2)]
    within = [(i, i + 1) for i in range(0, n - 1, 2)] + [(i + 1, i) for i in range(0, n - 1, 2)]
    got_across = lax.ppermute(jnp.where(odd, bottom, top), "tile", across)
    got_within = lax.ppermute(jnp.where(odd, top, bottom), "tile", within)
    low = jnp.where(odd, got_within, got_across)
    high = jnp.where(odd, got_across, got_within)
    return jnp.concatenate([low, block, high], axis=dim)


def shards(probe_signs, land_mask, kappa_sq, trait_covariance):
    rows = land_mask.shape[0]
    h = HALO
    signed = (land_mask[None, None] * (2 * probe_signs - 1)).astype(jnp.bfloat16)
    exchanged = lax.all_to_all(signed, "trait", split_axis=0, concat_axis=1, tiled=True)
    field_ext = halo_rows(exchanged, h).astype(jnp.float32)
    kappa_ext = halo_rows(kappa_sq, h)
    land_ext = field_ext[0, 0] * field_ext[0, 0]
    variances = jnp.diagonal(trait_covariance)
    z = field_ext * variances[None, :, None, None]

    def mix(x):
        return jnp.einsum("ts,psrc->ptrc", trait_covariance, x, precision=lax.Precision.HIGHEST)

    def stencil(x, off):
        r = x.shape[2]
        return land_ext[off + 1 : off + r - 1] * nine_valid(x, kappa_ext[off + 1 : off + r - 1])

    def apply_a(x, off):
        return mix(stencil(stencil(x, off), off + 1))

    def a_stages(x, off, split_mix=False):
        if split_mix:
            return (lambda _: stencil(x, off), lambda first: stencil(first, off + 1), mix)
        return (lambda _: stencil(x, off), lambda first: mix(stencil(first, off + 1)))

    def own(x, off):
        return x[:, :, h - off : h - off + rows]

    def lanes(v):
        return lax.optimization_barrier(jnp.broadcast_to(v[:, :, None], v.shape + (128,)))

    def crop(x, k):
        return x[:, :, k : x.shape[2] - k]

    def reduce_tile(pairs, off, work=()):
        prods = jnp.stack([own(a, off) * own(b, off) for a, b in pairs], axis=-1)
        return butterfly_sum(jnp.sum(prods, axis=(1, 2, 3)), "tile", work)

    az = apply_a(z, 0)
    z2 = crop(z, 2)
    sums, aaz = reduce_tile([(z2, z2), (az, z2)], 2, a_stages(az, 2, split_mix=True))
    sv = lanes(sums)
    norm_v = jnp.sqrt(sv[:, 0] + epsilon)
    alpha_v = sv[:, 1] / (norm_v * norm_v)
    norm = norm_v[:, 0]
    alpha = alpha_v[:, 0]
    q = z2 / norm[:, None, None, None]
    aq = az / norm[:, None, None, None]
    w = aq - alpha[:, None, None, None] * q
    aw = aaz / norm[:, None, None, None] - alpha[:, None, None, None] * crop(aq, 2)
    aq = crop(aq, 2)
    q = crop(q, 2)
    w = crop(w, 2)
    off = 4
    alphas = [alpha]
    betas = []
    iters = 3
    for step in range(1, iters):
        last_step = step == iters - 1
        sums, aaw = reduce_tile([(w, w), (aw, w), (q, w)], off, () if last_step else a_stages(aw, off))
        sv = lanes(sums)
        beta_v = jnp.sqrt(sv[:, 0] + epsilon)
        alpha_v = sv[:, 1] / (beta_v * beta_v) - sv[:, 2]
        beta = beta_v[:, 0]
        alpha = alpha_v[:, 0]
        q_next = w / beta[:, None, None, None]
        w_next = aw / beta[:, None, None, None] - beta[:, None, None, None] * q - alpha[:, None, None, None] * q_next
        if not last_step:
            aw_next = (
                aaw / beta[:, None, None, None]
                - beta[:, None, None, None] * crop(aq, 2)
                - alpha[:, None, None, None] * crop(aw, 2) / beta[:, None, None, None]
            )
            aq = crop(aw, 2) / beta[:, None, None, None]
            q = crop(q_next, 2)
            w = crop(w_next, 2)
            aw = aw_next
            off += 2
        else:
            q = q_next
            w = w_next
        betas.append(beta)
        alphas.append(alpha)
    w_own = own(w, off)
    w_back = lax.all_to_all(w_own, "trait", split_axis=1, concat_axis=0, tiled=True)
    partial = jnp.sum(w_own * w_own, axis=(1, 2, 3))[:, None]
    first = (lax.axis_index("tile") == 0).astype(jnp.float32)
    known = jnp.concatenate([jnp.stack(alphas, axis=1), jnp.stack(betas, axis=1)], axis=1)
    mine = jnp.concatenate([known * first, partial, norm[:, None] * first], axis=1)
    probes_local = mine.shape[0]
    n_trait = lax.axis_size("trait")
    owner = lax.broadcasted_iota(jnp.int32, (probes_local * n_trait, 1), 0) // probes_local
    spread = jnp.where(owner == lax.axis_index("trait"), jnp.tile(mine, (n_trait, 1)), 0.0)
    scalars = butterfly_sum(butterfly_sum(spread, "tile")[0], "trait")[0]
    tail = scalars[:, iters : 2 * iters]
    last_col = lax.broadcasted_iota(jnp.int32, tail.shape, 1) == iters - 1
    betas_all = jnp.where(last_col, jnp.sqrt(tail + epsilon), tail)
    beta = betas_all[:, iters - 1]
    norm_all = scalars[:, 2 * iters]
    last = (w_back / beta[:, None, None, None]) * norm_all[:, None, None, None]
    return scalars[:, :iters], betas_all, last


def solution(mesh):
    in_specs = (P(None, "trait", "tile", None), P("tile", None), P("tile", None), P())
    out_specs = (P(), P(), P(None, "trait", "tile", None))

    return jax.shard_map(shards, mesh=mesh, in_specs=in_specs, out_specs=out_specs, check_vma=False)
```

```python
import jax
import jax.numpy as jnp
from jax import lax
from jax.sharding import PartitionSpec as P


along_cols = 0.25
along_rows = 0.15
cross_term = 0.1
epsilon = 1e-06

HALO = 6


def nine_valid(x, kappa_rows):
    padded = jnp.pad(x, [(0, 0)] * (x.ndim - 1) + [(1, 1)])
    center = padded[..., 1:-1, 1:-1]
    sideways = padded[..., 1:-1, :-2] + padded[..., 1:-1, 2:]
    vertical = padded[..., :-2, 1:-1] + padded[..., 2:, 1:-1]
    diag_main = padded[..., 2:, 2:] + padded[..., :-2, :-2]
    diag_anti = padded[..., 2:, :-2] + padded[..., :-2, 2:]
    return (
        (kappa_rows + 2.0 * along_cols + 2.0 * along_rows) * center
        - along_cols * sideways
        - along_rows * vertical
        - 0.5 * cross_term * (diag_main - diag_anti)
    )


def butterfly_sum(v, axis, work=()):
    n = lax.axis_size(axis)
    carry = None
    if n & (n - 1):
        for stage in work:
            carry = stage(carry)
        return lax.psum(v, axis), carry
    s = 1
    r = 0
    while s < n:
        got = lax.ppermute(v, axis, [(i, i ^ s) for i in range(n)])
        if r < len(work):
            carry = work[r](carry)
            v, carry = lax.optimization_barrier((v + got, carry))
        else:
            v = v + got
        s *= 2
        r += 1
    for stage in work[r:]:
        carry = stage(carry)
    return v, carry


def halo_rows(block, width):
    n = lax.axis_size("tile")
    dim = block.ndim - 2
    rows = block.shape[dim]
    assert rows >= width and n % 2 == 0
    top = lax.slice_in_dim(block, 0, width, axis=dim)
    bottom = lax.slice_in_dim(block, rows - width, rows, axis=dim)
    odd = lax.axis_index("tile") % 2 == 1
    across = [(i, i + 1) for i in range(1, n - 1, 2)] + [(i + 1, i) for i in range(1, n - 1, 2)]
    within = [(i, i + 1) for i in range(0, n - 1, 2)] + [(i + 1, i) for i in range(0, n - 1, 2)]
    got_across = lax.ppermute(jnp.where(odd, bottom, top), "tile", across)
    got_within = lax.ppermute(jnp.where(odd, top, bottom), "tile", within)
    low = jnp.where(odd, got_within, got_across)
    high = jnp.where(odd, got_across, got_within)
    return jnp.concatenate([low, block, high], axis=dim)


def shards(probe_signs, land_mask, kappa_sq, trait_covariance):
    rows = land_mask.shape[0]
    h = HALO
    signed = (land_mask[None, None] * (2 * probe_signs - 1)).astype(jnp.bfloat16)
    exchanged = lax.all_to_all(signed, "trait", split_axis=0, concat_axis=1, tiled=True)
    field_ext = halo_rows(exchanged, h).astype(jnp.float32)
    kappa_ext = halo_rows(kappa_sq, h)
    land_ext = field_ext[0, 0] * field_ext[0, 0]
    variances = jnp.diagonal(trait_covariance)
    z = field_ext * variances[None, :, None, None]

    def mix(x):
        return jnp.einsum("ts,psrc->ptrc", trait_covariance, x, precision=lax.Precision.HIGHEST)

    def stencil(x, off):
        r = x.shape[2]
        return land_ext[off + 1 : off + r - 1] * nine_valid(x, kappa_ext[off + 1 : off + r - 1])

    def apply_a(x, off):
        return mix(stencil(stencil(x, off), off + 1))

    def a_stages(x, off, split_mix=False):
        if split_mix:
            return (lambda _: stencil(x, off), lambda first: stencil(first, off + 1), mix)
        return (lambda _: stencil(x, off), lambda first: mix(stencil(first, off + 1)))

    def own(x, off):
        return x[:, :, h - off : h - off + rows]

    def lanes(v):
        return lax.optimization_barrier(jnp.broadcast_to(v[:, :, None], v.shape + (128,)))

    def crop(x, k):
        return x[:, :, k : x.shape[2] - k]

    def reduce_tile(pairs, off, work=()):
        prods = jnp.stack([own(a, off) * own(b, off) for a, b in pairs], axis=-1)
        return butterfly_sum(jnp.sum(prods, axis=(1, 2, 3)), "tile", work)

    az = apply_a(z, 0)
    z2 = crop(z, 2)
    sums, aaz = reduce_tile([(z2, z2), (az, z2)], 2, a_stages(az, 2, split_mix=True))
    sv = lanes(sums)
    norm_v = jnp.sqrt(sv[:, 0] + epsilon)
    alpha_v = sv[:, 1] / (norm_v * norm_v)
    norm = norm_v[:, 0]
    alpha = alpha_v[:, 0]
    q = z2 / norm[:, None, None, None]
    aq = az / norm[:, None, None, None]
    w = aq - alpha[:, None, None, None] * q
    aw = aaz / norm[:, None, None, None] - alpha[:, None, None, None] * crop(aq, 2)
    aq = crop(aq, 2)
    q = crop(q, 2)
    w = crop(w, 2)
    off = 4
    alphas = [alpha]
    betas = []
    iters = 3
    for step in range(1, iters):
        last_step = step == iters - 1
        sums, aaw = reduce_tile([(w, w), (aw, w), (q, w)], off, () if last_step else a_stages(aw, off))
        sv = lanes(sums)
        beta_v = jnp.sqrt(sv[:, 0] + epsilon)
        alpha_v = sv[:, 1] / (beta_v * beta_v) - sv[:, 2]
        beta = beta_v[:, 0]
        alpha = alpha_v[:, 0]
        q_next = w / beta[:, None, None, None]
        w_next = aw / beta[:, None, None, None] - beta[:, None, None, None] * q - alpha[:, None, None, None] * q_next
        if not last_step:
            aw_next = (
                aaw / beta[:, None, None, None]
                - beta[:, None, None, None] * crop(aq, 2)
                - alpha[:, None, None, None] * crop(aw, 2) / beta[:, None, None, None]
            )
            aq = crop(aw, 2) / beta[:, None, None, None]
            q = crop(q_next, 2)
            w = crop(w_next, 2)
            aw = aw_next
            off += 2
        else:
            q = q_next
            w = w_next
        betas.append(beta)
        alphas.append(alpha)
    w_own = own(w, off)
    w_back = lax.all_to_all(w_own, "trait", split_axis=1, concat_axis=0, tiled=True)
    partial = jnp.sum(w_own * w_own, axis=(1, 2, 3))[:, None]
    first = (lax.axis_index("tile") == 0).astype(jnp.float32)
    known = jnp.concatenate([jnp.stack(alphas, axis=1), jnp.stack(betas, axis=1)], axis=1)
    mine = jnp.concatenate([known * first, partial, norm[:, None] * first], axis=1)
    probes_local = mine.shape[0]
    n_trait = lax.axis_size("trait")
    spread = lax.dynamic_update_slice(
        jnp.zeros((probes_local * n_trait, mine.shape[1]), jnp.float32),
        mine,
        (lax.axis_index("trait") * probes_local, 0),
    )
    scalars = butterfly_sum(butterfly_sum(spread, "tile")[0], "trait")[0]
    tail = scalars[:, iters : 2 * iters]
    last_col = lax.broadcasted_iota(jnp.int32, tail.shape, 1) == iters - 1
    betas_all = jnp.where(last_col, jnp.sqrt(tail + epsilon), tail)
    beta = betas_all[:, iters - 1]
    norm_all = scalars[:, 2 * iters]
    last = (w_back / beta[:, None, None, None]) * norm_all[:, None, None, None]
    return scalars[:, :iters], betas_all, last


def solution(mesh):
    in_specs = (P(None, "trait", "tile", None), P("tile", None), P("tile", None), P())
    out_specs = (P(), P(), P(None, "trait", "tile", None))

    return jax.shard_map(shards, mesh=mesh, in_specs=in_specs, out_specs=out_specs, check_vma=False)
```
